32 devices in a mesh: grp: 4 (over x, core), tp: 8 (over z, y).
Axes of the slice: x: 2, y: 2, z: 4, core: 2. Of those that a mesh axis runs over, the one named last changes fastest.
Arguments:
- hidden_in: bfloat16 [3072, 3584], P('grp'), may hold values from -6 to 6
- lengths: int32 [8, 8], P('grp'), may hold values from 1 to 96, 384 in all within a row
- dest: int32 [64, 1], P('grp'), may hold values from 0 to 3; in each aligned block of 16 rows (0 to 15, 16 to 31, ...) at most 4 rows name the same one
- attn_gain: float32 [3584], replicated, may hold values from 0.6 to 8
- q_weight: bfloat16 [3584, 2048], P('grp', 'tp'), may hold values from -0.09375 to 0.09375
- k_weight: bfloat16 [3584, 512], P('grp', 'tp'), may hold values from -0.09375 to 0.09375
- v_weight: bfloat16 [3584, 512], P('grp', 'tp'), may hold values from -0.09375 to 0.09375
- o_weight: bfloat16 [3584, 2048], P('grp', 'tp'), may hold values from -0.125 to 0.125
- ffn_gain: float32 [3584], replicated, may hold values from 0.1 to 1.9
- gate_weight: bfloat16 [3584, 10240], P('grp', 'tp'), may hold values from -0.09375 to 0.09375
- up_weight: bfloat16 [3584, 10240], P('grp', 'tp'), may hold values from -0.09375 to 0.09375
- down_weight: bfloat16 [3584, 10240], P('grp', 'tp'), may hold values from -0.0625 to 0.0625
Outputs:
- bank_in: bfloat16 [4, 4, 4, 3584], P('grp', None, None, 'tp')
The draws below stay inside these ranges and needn't reach their ends.
Inputs may be any that keep to these rules, and one draw needn't show every extreme that they name: Each block's 8 lengths sum to 384. `dest`: among the programs of one index of grp, no bank shard is named by more than 4.
All inputs are finite; a program needn't handle non-finite values.
Results may differ from the reference program's by a relative error of at most 0.015.
The reference program's roundings to bfloat16 on the way count: a program that leaves them out, or rounds other values in their place, can miss the bound.
Values may be sent and summed in bfloat16 or wider, within the bound.
No kernel may reach another device: no remote copies, remote signals or barrier semaphores. Data moves between devices by JAX's collectives and lax.ppermute only.
A program may use at most 128 MiB of HBM per device.

```python
import math
import jax
import jax.numpy as jnp
import numpy as np
from jax import lax

D = 3584
HEAD_SIZE = 128
KVH = 4
HEADS = 16
FF = 10240
BLK = 384
PPB = 8
LMAX = 96
PROGS_DEV = 16
CAP = 4
NBLK = 8
ROWS = 3072
PROGS = 64
N_GRP = 4
N_TP = 8


def draw_attn_gain(key, part):
    return jax.random.uniform(key, (D,), jnp.float32, 0.6, 1.4)


def shard_levels(key, shape, pieces, least, largest):
    loudness, own = 1.0, jax.random.fold_in(key, 6)
    for dim, parts in pieces:
        draws = jnp.exp(jax.random.uniform(jax.random.fold_in(own, dim), (parts,), jnp.float32, least / len(pieces), largest / len(pieces)))
        loudness = loudness * jnp.repeat(draws, shape[dim] // parts).reshape([-1 if axis == dim else 1 for axis in range(len(shape))])
    return loudness


def profile(number_of, total, most, slope):
    weights = [(1 << 20) // math.isqrt(standing ** slope) + 1 for standing in range(2, number_of + 1)]
    spare, holding = total - most - (number_of - 1), [1] * (number_of - 1)
    while spare > 0:
        candidates = [i for i in range(number_of - 1) if holding[i] < most]
        mass, budget = sum([weights[i] for i in candidates]), spare
        for i in candidates:
            addition = min(most - holding[i], max(1, budget * weights[i] // mass), spare)
            holding[i] = holding[i] + addition
            spare = spare - addition
    return np.array([most] + holding)


def ragged(key, amount, total, limit, slope):
    if amount == 2:
        one = jax.random.randint(key, (), max(1, total - limit), min(limit, total - 1) + 1)
        return jnp.stack([one, total - one])
    sizes = jnp.asarray(profile(amount, total, limit, slope), jnp.int32)
    twos = (amount - 1) // 2
    giver, taker = sizes[1:1 + 2 * twos:2], sizes[2:2 + 2 * twos:2]
    margin = jnp.minimum(giver - 1, limit - taker)
    shifted = jax.random.randint(jax.random.fold_in(key, 1), (twos,), 0, 1 << 20) % (margin + 1)
    sizes = sizes.at[1:1 + 2 * twos:2].set(giver - shifted).at[2:2 + 2 * twos:2].set(taker + shifted)
    return sizes[jax.random.permutation(jax.random.fold_in(key, 2), amount)]


def shared_out(key, own, number, rows, amount, top, most, lean):
    ranking = jax.random.permutation(key, amount)
    packed, common = shares(amount, rows * top, most, lean, True), shares(amount, rows * top, most, lean, False)
    places = jnp.arange(amount)

    def named(sizes, turn):
        used = int((sizes > 0).sum())
        fixed = max(1, used // 4)
        moved = fixed + (places - fixed + turn * (used - fixed)) % max(1, amount - fixed)
        return jnp.zeros((amount,), jnp.int32).at[ranking[jnp.where(places < fixed, places, moved)]].set(jnp.asarray(sizes, jnp.int32))

    sizes = jnp.where(number % 4 == 0, named(packed, number // 4), named(common, number - number // 4 - 1))
    mixed = jax.random.permutation(jax.random.fold_in(own, 3), amount)
    source_of, taker = mixed[0:amount // 2 * 2:2], mixed[1:amount // 2 * 2:2]
    room = jnp.minimum(sizes[source_of] - 1, most - sizes[taker]) // 2
    room = jnp.where((source_of == ranking[0]) | (taker == ranking[0]) | (sizes[taker] == 0), 0, jnp.maximum(room, 0))
    moved = jax.random.randint(jax.random.fold_in(own, 4), (amount // 2,), 0, 1 << 20) % (room + 1)
    sizes = sizes.at[source_of].add(-moved).at[taker].add(moved)
    members = jnp.searchsorted(jnp.cumsum(sizes), jnp.arange(rows * top), side="right").astype(jnp.int32)
    grid = members.reshape(top, rows).T
    grid = grid[jax.random.permutation(jax.random.fold_in(own, 1), rows)]
    turn = jax.random.randint(jax.random.fold_in(own, 2), (rows, 1), 0, top)
    return jnp.take_along_axis(grid, (jnp.arange(top)[None, :] + turn) % top, axis=1)


def shares(amount, total, limit, slope, full):
    portions = [(1 << 20) // math.isqrt(grade ** slope) + 1 for grade in range(1, amount + 1)]
    largest = limit if full else min(limit, max(-(-total // amount), total * portions[0] // sum(portions)))
    least = 1 if total - largest >= amount - 1 else 0
    given, rest = [largest] + [least] * (amount - 1), total - largest - least * (amount - 1)
    while rest > 0:
        movable = [i for i in range(1, amount) if given[i] < largest] or [i for i in range(1, amount) if given[i] < limit]
        whole, remaining = sum([portions[i] for i in movable]), rest
        for i in movable:
            more = min(limit - given[i], max(1, remaining * portions[i] // whole), rest)
            given[i] = given[i] + more
            rest = rest - more
    return np.array(given)


def normal_values(rng, shape, deviation, reach, shards=(), held_as=jnp.bfloat16):
    entries = deviation * jax.random.normal(rng, shape, jnp.float32)
    if shards:
        entries = entries * shard_levels(rng, shape, shards, -0.22, 0.18)
    return jnp.clip(entries, -reach, reach).astype(held_as)


def setup_inputs(seed: int = 0) -> dict:
    keys = jax.random.split(jax.random.key(seed), 13)
    hidden_in = normal_values(keys[0], (ROWS, D), 1.0, 6.0, ((0, 4),))
    lengths = jax.vmap(lambda own: ragged(own, PPB, BLK, LMAX, 1))(jax.random.split(keys[1], NBLK)).reshape((NBLK, PPB)).astype(jnp.int32)
    dest_keys = jax.random.split(jax.random.fold_in(keys[2], 1), PROGS // PROGS_DEV)
    dest_turns = jax.random.permutation(jax.random.fold_in(keys[2], 3), PROGS // PROGS_DEV)
    dest = jax.vmap(lambda own, number: shared_out(jax.random.fold_in(keys[2], 2), own, number, PROGS_DEV, N_GRP, 1, CAP, 2))(dest_keys, dest_turns).reshape((PROGS, 1))
    attn_gain = draw_attn_gain(jax.random.fold_in(keys[12], 71), 0)
    q_weight = normal_values(keys[4], (D, HEADS * HEAD_SIZE), D ** -0.5, 0.09375, ((0, 4), (1, 8)))
    k_weight = normal_values(keys[5], (D, KVH * HEAD_SIZE), D ** -0.5, 0.09375, ((0, 4), (1, 8)))
    v_weight = normal_values(keys[6], (D, KVH * HEAD_SIZE), D ** -0.5, 0.09375, ((0, 4), (1, 8)))
    o_weight = normal_values(keys[7], (D, HEADS * HEAD_SIZE), (HEADS * HEAD_SIZE) ** -0.5, 0.125, ((0, 4), (1, 8)))
    ffn_gain = jnp.clip(1.0 + 0.18 * jax.random.normal(keys[8], (D,), jnp.float32), 0.1, 1.9)
    gate_weight = normal_values(keys[9], (D, FF), D ** -0.5, 0.09375, ((0, 4), (1, 8)))
    up_weight = normal_values(keys[10], (D, FF), D ** -0.5, 0.09375, ((0, 4), (1, 8)))
    down_weight = normal_values(keys[11], (D, FF), FF ** -0.5, 0.0625, ((0, 4), (1, 8)))
    return {"hidden_in": hidden_in, "lengths": lengths, "dest": dest, "attn_gain": attn_gain, "q_weight": q_weight, "k_weight": k_weight, "v_weight": v_weight, "o_weight": o_weight, "ffn_gain": ffn_gain, "gate_weight": gate_weight, "up_weight": up_weight, "down_weight": down_weight}


EPSILON = 1e-06
HIGH = lax.Precision.HIGHEST

def rms_scale(rows, gain):
    rows = rows.astype(jnp.float32)
    factor = lax.rsqrt(lax.optimization_barrier(jnp.mean(rows * rows, axis=1, keepdims=True)) + EPSILON)
    return (rows * factor * gain[None, :]).astype(jnp.bfloat16)

def segment_ids(lengths, block_rows):
    bounds = jnp.cumsum(lengths, axis=1)
    position = lax.broadcasted_iota(jnp.int32, (lengths.shape[0], block_rows), 1)
    return lax.optimization_barrier(jnp.sum((position[:, :, None] >= bounds[:, None, :]).astype(jnp.int32), axis=2))

def softmax_rows(attention_scores):
    top = lax.optimization_barrier(jnp.max(attention_scores, axis=-1, keepdims=True))
    expo = jnp.exp(attention_scores - top)
    return (expo / lax.optimization_barrier(jnp.sum(expo, axis=-1, keepdims=True))).astype(jnp.bfloat16)

def reference(hidden_in, lengths, dest, attn_gain, q_weight, k_weight, v_weight, o_weight, ffn_gain, gate_weight, up_weight, down_weight):
    rows_all = hidden_in.shape[0]
    norm_in = rms_scale(hidden_in, attn_gain)
    queries = jnp.dot(norm_in, q_weight, preferred_element_type=jnp.float32).astype(jnp.bfloat16)
    keys_all = jnp.dot(norm_in, k_weight, preferred_element_type=jnp.float32).astype(jnp.bfloat16)
    vals_all = jnp.dot(norm_in, v_weight, preferred_element_type=jnp.float32).astype(jnp.bfloat16)
    keys_split = keys_all.reshape(rows_all, HEAD_SIZE, KVH)
    vals_split = vals_all.reshape(rows_all, HEAD_SIZE, KVH)
    segs = segment_ids(lengths, BLK)
    same = segs[:, :, None] == segs[:, None, :]
    local_heads = HEADS // N_TP
    group_heads = HEADS // KVH
    attn_total = jnp.zeros((rows_all, D), jnp.float32)
    for tp_slot in range(N_TP):
        head_low = tp_slot * local_heads
        kv_index = head_low // group_heads
        blocked_queries = queries[:, head_low * HEAD_SIZE:(head_low + local_heads) * HEAD_SIZE].reshape(NBLK, BLK, local_heads, HEAD_SIZE)
        blocked_keys = keys_split[:, :, kv_index].reshape(NBLK, BLK, HEAD_SIZE)
        blocked_values = vals_split[:, :, kv_index].reshape(NBLK, BLK, HEAD_SIZE)
        attention_scores = jnp.einsum('xwre,xpe->xrwp', blocked_queries.astype(jnp.float32), blocked_keys.astype(jnp.float32)) * HEAD_SIZE ** (-0.5)
        attention_scores = jnp.where(same[:, None, :, :], attention_scores, -1e+30)
        attention_probabilities = softmax_rows(attention_scores)
        attended_rows = jnp.einsum('asfo,aon->afsn', attention_probabilities.astype(jnp.float32), blocked_values.astype(jnp.float32))
        attended_rows = attended_rows.astype(jnp.bfloat16).reshape(rows_all, local_heads * HEAD_SIZE)
        columns = o_weight[:, head_low * HEAD_SIZE:(head_low + local_heads) * HEAD_SIZE]
        term = lax.dot_general(attended_rows, columns, (((1,), (1,)), ((), ())), preferred_element_type=jnp.float32)
        attn_total = attn_total + lax.optimization_barrier(term.astype(jnp.bfloat16)).astype(jnp.float32)
    residual = hidden_in.astype(jnp.float32) + attn_total
    norm_mid = rms_scale(residual, ffn_gain)
    ffn_width = FF // N_TP
    ffn_total = jnp.zeros((rows_all, D), jnp.float32)
    for tp_slot in range(N_TP):
        low = tp_slot * ffn_width
        gate_pre = jnp.dot(norm_mid, gate_weight[:, low:low + ffn_width], preferred_element_type=jnp.float32)
        up_pre = jnp.dot(norm_mid, up_weight[:, low:low + ffn_width], preferred_element_type=jnp.float32)
        hidden_ffn = (jax.nn.silu(gate_pre) * up_pre).astype(jnp.bfloat16)
        term = lax.dot_general(hidden_ffn, down_weight[:, low:low + ffn_width], (((1,), (1,)), ((), ())), preferred_element_type=jnp.float32)
        ffn_total = ffn_total + lax.optimization_barrier(term.astype(jnp.bfloat16)).astype(jnp.float32)
    layer_out = (residual + ffn_total).reshape(NBLK, BLK, D)
    program_ids = lax.broadcasted_iota(jnp.int32, (NBLK, PPB, BLK), 1)
    selector = (segs[:, None, :] == program_ids).astype(jnp.float32)
    sums = jnp.einsum('bjr,brd->bjd', selector, layer_out, precision=HIGH).reshape(PROGS, D)
    counts = lengths.reshape(PROGS).astype(jnp.float32)
    pooled = (sums / counts[:, None]).astype(jnp.bfloat16)
    targets = dest[:, 0].reshape(N_GRP, PROGS_DEV)
    grp_ids = lax.broadcasted_iota(jnp.int32, (N_GRP, PROGS_DEV, N_GRP), 2)
    chosen = (targets[:, :, None] == grp_ids).astype(jnp.int32)
    earlier = jnp.cumsum(chosen, axis=1) - chosen
    slot_rank = lax.optimization_barrier(jnp.sum(earlier * chosen, axis=2))
    slot_ids = targets * CAP + slot_rank
    slot_grid = lax.broadcasted_iota(jnp.int32, (N_GRP, N_GRP * CAP, PROGS_DEV), 1)
    placer = (slot_grid == slot_ids[:, None, :]).astype(jnp.float32)
    embedded = pooled.astype(jnp.float32).reshape(N_GRP, PROGS_DEV, D)
    outgoing = jnp.einsum('smp,spd->smd', placer, embedded, precision=HIGH)
    bank_in = outgoing.reshape(N_GRP, N_GRP, CAP, D).transpose(1, 0, 2, 3)
    return bank_in.astype(jnp.bfloat16)
```

```python
import jax
import jax.numpy as jnp
from jax import lax
from jax.sharding import PartitionSpec as P

HEAD_SIZE = 128
KVH = 4
HEADS = 16


EPSILON = 1e-06
HIGH = lax.Precision.HIGHEST


def rms_scale(rows, gain):
    rows = rows.astype(jnp.float32)
    factor = lax.rsqrt(jnp.mean(rows * rows, axis=1, keepdims=True) + EPSILON)
    return (rows * factor * gain[None, :]).astype(jnp.bfloat16)


def segment_ids(lengths, block_rows):
    bounds = jnp.cumsum(lengths, axis=1)
    position = lax.broadcasted_iota(jnp.int32, (lengths.shape[0], block_rows), 1)
    return jnp.sum((position[:, :, None] >= bounds[:, None, :]).astype(jnp.int32), axis=2)


def softmax_rows(attention_scores):
    top = jnp.max(attention_scores, axis=-1, keepdims=True)
    expo = jnp.exp(attention_scores - top)
    return (expo / jnp.sum(expo, axis=-1, keepdims=True)).astype(jnp.bfloat16)


def transposed_dot(left, right):
    return lax.dot_general(
        left, right, (((1,), (1,)), ((), ())), preferred_element_type=jnp.float32
    )


def gather_grp(piece, chips):
    held = [piece]
    moving = piece
    if chips > 1:
        ring = [(2 * i + c, 2 * ((i + 1) % chips) + c) for i in range(chips) for c in range(2)]
        for _ in range(chips - 1):
            moving = lax.ppermute(moving, "grp", ring)
            held.append(moving)
    mine = jnp.stack(held)
    other = lax.ppermute(mine, "grp", [(g, g ^ 1) for g in range(2 * chips)])
    return jnp.concatenate([mine, other], 0)


def source_order(chips):
    g = lax.axis_index("grp")
    chip, core = g // 2, g % 2
    steps = jnp.arange(chips, dtype=jnp.int32)
    own = 2 * ((chip - steps) % chips) + core
    return jnp.concatenate([own, own - core + (1 - core)])


def take_blocks(x, order, size, axis):
    return jnp.concatenate(
        [lax.dynamic_slice_in_dim(x, order[k] * size, size, axis) for k in range(order.shape[0])],
        axis,
    )


def on_device(
    hidden_in,
    lengths,
    dest,
    attn_gain,
    q_weight,
    k_weight,
    v_weight,
    o_weight,
    ffn_gain,
    gate_weight,
    up_weight,
    down_weight,
):
    row_count, width = hidden_in.shape
    blocks, per_block = lengths.shape
    block_rows = row_count // blocks
    programs = blocks * per_block
    tp_size = lax.axis_size("tp")
    grp_size = lax.axis_size("grp")
    chips = grp_size // 2
    tp_index = lax.axis_index("tp")
    grp_index = lax.axis_index("grp")
    d_grp = width // grp_size
    d_tp = width // tp_size
    ratio = tp_size // grp_size
    capacity = max(2, (programs + grp_size - 1) // grp_size)
    local_heads = q_weight.shape[1] // HEAD_SIZE
    order = source_order(chips)

    q_cols, k_cols = q_weight.shape[1], k_weight.shape[1]
    qkv_full = gather_grp(jnp.concatenate([q_weight, k_weight, v_weight], 1), chips)
    qkv_full = qkv_full.reshape(width, -1)
    o_full = gather_grp(o_weight, chips).reshape(width, -1)
    gate_full = gather_grp(gate_weight, chips).reshape(width, -1)
    up_full = gather_grp(up_weight, chips).reshape(width, -1)

    hidden_perm = take_blocks(hidden_in, order, d_grp, 1)
    attn_gain_perm = take_blocks(attn_gain, order, d_grp, 0)
    ffn_gain_perm = take_blocks(ffn_gain, order, d_grp, 0)

    norm_in = rms_scale(hidden_perm, attn_gain_perm)
    qkv = jnp.dot(norm_in, qkv_full, preferred_element_type=jnp.float32).astype(jnp.bfloat16)
    queries = qkv[:, :q_cols]
    kv_part = qkv[:, q_cols:]
    kv_all = lax.all_to_all(
        jnp.broadcast_to(kv_part[None], (tp_size,) + kv_part.shape), "tp", 0, 0, tiled=True
    )
    per_dev = k_cols // KVH
    kv_index = tp_index * local_heads // (HEADS // KVH)

    def head_of(part):
        split = part.reshape(tp_size, row_count, per_dev, KVH)
        one = lax.dynamic_slice_in_dim(split, kv_index, 1, 3)[..., 0]
        return one.transpose(1, 0, 2).reshape(row_count, tp_size * per_dev)

    key_head = head_of(kv_all[:, :, :k_cols])
    value_head = head_of(kv_all[:, :, k_cols:])

    segs = segment_ids(lengths, block_rows)
    same = segs[:, :, None] == segs[:, None, :]
    blocked_queries = queries.reshape(blocks, block_rows, local_heads, HEAD_SIZE)
    blocked_keys = key_head.reshape(blocks, block_rows, HEAD_SIZE)
    blocked_values = value_head.reshape(blocks, block_rows, HEAD_SIZE)
    attention_scores = jnp.einsum(
        "xwre,xpe->xrwp", blocked_queries, blocked_keys, preferred_element_type=jnp.float32
    ) * HEAD_SIZE ** (-0.5)
    attention_scores = jnp.where(same[:, None, :, :], attention_scores, -1e30)
    attention_probabilities = softmax_rows(attention_scores)
    attended_rows = jnp.einsum(
        "asfo,aon->afsn",
        attention_probabilities,
        blocked_values,
        preferred_element_type=jnp.float32,
    )
    attended_rows = attended_rows.astype(jnp.bfloat16).reshape(row_count, local_heads * HEAD_SIZE)
    attn_term = transposed_dot(attended_rows, o_full)
    attn_total = lax.psum(attn_term.astype(jnp.bfloat16), "tp").astype(jnp.float32)
    residual = hidden_perm.astype(jnp.float32) + attn_total
    norm_mid = rms_scale(residual, ffn_gain_perm)
    gate_pre = jnp.dot(norm_mid, gate_full, preferred_element_type=jnp.float32)
    up_pre = jnp.dot(norm_mid, up_full, preferred_element_type=jnp.float32)
    hidden_ffn = (jax.nn.silu(gate_pre) * up_pre).astype(jnp.bfloat16)

    block_index = lax.broadcasted_iota(jnp.int32, (blocks, block_rows), 0)
    program_of_row = (block_index * per_block + segs).reshape(row_count)
    program_grid = lax.broadcasted_iota(jnp.int32, (programs, row_count), 0)
    selector = (program_grid == program_of_row[None, :]).astype(jnp.float32)
    hidden_sums = jnp.dot(
        selector.astype(jnp.bfloat16), hidden_ffn, preferred_element_type=jnp.float32
    )
    chunk_owner = tp_index // ratio
    owner_step = jnp.argmax(order == chunk_owner).astype(jnp.int32)
    chunk_start = owner_step * d_grp + (tp_index % ratio) * d_tp
    residual_chunk = lax.dynamic_slice_in_dim(residual, chunk_start, d_tp, 1)
    residual_sums = jnp.dot(selector, residual_chunk, precision=HIGH, preferred_element_type=jnp.float32)

    hidden_all = gather_grp(hidden_sums, chips).reshape(grp_size * programs, -1)
    down_part = lax.dot_general(
        hidden_all, down_weight.astype(jnp.float32), (((1,), (1,)), ((), ())),
        precision=HIGH, preferred_element_type=jnp.float32,
    )

    dest_all = gather_grp(dest[:, 0], chips)
    lengths_all = gather_grp(lengths.reshape(programs), chips).reshape(grp_size * programs)
    grp_ids = lax.broadcasted_iota(jnp.int32, (grp_size, programs, grp_size), 2)
    chosen = (dest_all[:, :, None] == grp_ids).astype(jnp.int32)
    earlier = jnp.cumsum(chosen, axis=1) - chosen
    slot_rank = jnp.sum(earlier * chosen, axis=2)
    slot_row = order[:, None] * capacity + slot_rank
    slots = grp_size * capacity
    target_grid = lax.broadcasted_iota(jnp.int32, (grp_size, slots, grp_size, programs), 0)
    row_grid = lax.broadcasted_iota(jnp.int32, (grp_size, slots, grp_size, programs), 1)
    placer = (
        (target_grid == dest_all[None, None]) & (row_grid == slot_row[None, None])
    ).astype(jnp.float32).reshape(grp_size, slots, grp_size * programs)
    down_slots = jnp.einsum("asq,qd->asd", placer, down_part, precision=HIGH)
    down_slots = down_slots.reshape(grp_size, slots, ratio, d_tp).transpose(0, 2, 1, 3)
    send = lax.dynamic_update_slice(
        jnp.zeros((grp_size, tp_size, slots, d_tp), jnp.float32),
        down_slots,
        (0, grp_index * ratio, 0, 0),
    )
    local_placer = placer[:, :, :programs]
    residual_slots = jnp.einsum("asq,qd->asd", local_placer, residual_sums, precision=HIGH)
    send = send + lax.dynamic_update_slice(
        jnp.zeros((grp_size, tp_size, slots, d_tp), jnp.float32),
        residual_slots[:, None],
        (0, tp_index, 0, 0),
    )
    received = lax.all_to_all(
        send.reshape(grp_size * tp_size, slots, d_tp), ("grp", "tp"), 0, 0, tiled=True
    )
    totals = jnp.sum(received, axis=0)
    mine = lax.dynamic_index_in_dim(placer, grp_index, 0, keepdims=False)
    counts = jnp.dot(mine, lengths_all.astype(jnp.float32), precision=HIGH)
    counts = jnp.where(counts > 0, counts, 1.0)
    embedded = (totals / counts[:, None]).astype(jnp.bfloat16)
    return embedded.reshape(1, grp_size, capacity, d_tp)


def solution(mesh):
    placed = (
        P("grp", None),
        P("grp", None),
        P("grp", None),
        P(),
        P("grp", "tp"),
        P("grp", "tp"),
        P("grp", "tp"),
        P("grp", "tp"),
        P(),
        P("grp", "tp"),
        P("grp", "tp"),
        P("grp", "tp"),
    )
    return jax.shard_map(
        on_device, mesh=mesh, in_specs=placed, out_specs=P("grp", None, None, "tp"), check_vma=False
    )
```

```python
import jax
import jax.numpy as jnp
from jax import lax
from jax.sharding import PartitionSpec as P

HEAD_SIZE = 128
KVH = 4
HEADS = 16


EPSILON = 1e-06
HIGH = lax.Precision.HIGHEST


def rms_scale(rows, gain):
    rows = rows.astype(jnp.float32)
    factor = lax.rsqrt(jnp.mean(rows * rows, axis=1, keepdims=True) + EPSILON)
    return (rows * factor * gain[None, :]).astype(jnp.bfloat16)


def segment_ids(lengths, block_rows):
    bounds = jnp.cumsum(lengths, axis=1)
    position = lax.broadcasted_iota(jnp.int32, (lengths.shape[0], block_rows), 1)
    return jnp.sum((position[:, :, None] >= bounds[:, None, :]).astype(jnp.int32), axis=2)


def softmax_rows(attention_scores):
    top = jnp.max(attention_scores, axis=-1, keepdims=True)
    expo = jnp.exp(attention_scores - top)
    return (expo / jnp.sum(expo, axis=-1, keepdims=True)).astype(jnp.bfloat16)


def transposed_dot(left, right):
    return lax.dot_general(
        left, right, (((1,), (1,)), ((), ())), preferred_element_type=jnp.float32
    )


def gather_grp(piece, chips):
    held = [piece]
    moving = piece
    if chips > 1:
        ring = [(2 * i + c, 2 * ((i + 1) % chips) + c) for i in range(chips) for c in range(2)]
        for _ in range(chips - 1):
            moving = lax.ppermute(moving, "grp", ring)
            held.append(moving)
    mine = jnp.stack(held)
    other = lax.ppermute(mine, "grp", [(g, g ^ 1) for g in range(2 * chips)])
    return jnp.concatenate([mine, other], 0)


def source_order(chips):
    g = lax.axis_index("grp")
    chip, core = g // 2, g % 2
    steps = jnp.arange(chips, dtype=jnp.int32)
    own = 2 * ((chip - steps) % chips) + core
    return jnp.concatenate([own, own - core + (1 - core)])


def take_blocks(x, order, size, axis):
    return jnp.concatenate(
        [lax.dynamic_slice_in_dim(x, order[k] * size, size, axis) for k in range(order.shape[0])],
        axis,
    )


def on_device(
    hidden_in,
    lengths,
    dest,
    attn_gain,
    q_weight,
    k_weight,
    v_weight,
    o_weight,
    ffn_gain,
    gate_weight,
    up_weight,
    down_weight,
):
    row_count, width = hidden_in.shape
    blocks, per_block = lengths.shape
    block_rows = row_count // blocks
    programs = blocks * per_block
    tp_size = lax.axis_size("tp")
    grp_size = lax.axis_size("grp")
    chips = grp_size // 2
    tp_index = lax.axis_index("tp")
    grp_index = lax.axis_index("grp")
    d_grp = width // grp_size
    d_tp = width // tp_size
    ratio = tp_size // grp_size
    capacity = max(2, (programs + grp_size - 1) // grp_size)
    local_heads = q_weight.shape[1] // HEAD_SIZE
    order = source_order(chips)

    q_cols, k_cols = q_weight.shape[1], k_weight.shape[1]
    qkv_full = gather_grp(jnp.concatenate([q_weight, k_weight, v_weight], 1), chips)
    qkv_full = qkv_full.reshape(width, -1)
    o_after, qkv_full = lax.optimization_barrier((o_weight, qkv_full))
    o_full = gather_grp(o_after, chips).reshape(width, -1)
    gate_after, up_after, o_full = lax.optimization_barrier((gate_weight, up_weight, o_full))
    gate_full = gather_grp(gate_after, chips).reshape(width, -1)
    up_full = gather_grp(up_after, chips).reshape(width, -1)

    hidden_perm = take_blocks(hidden_in, order, d_grp, 1)
    attn_gain_perm = take_blocks(attn_gain, order, d_grp, 0)
    ffn_gain_perm = take_blocks(ffn_gain, order, d_grp, 0)

    norm_in = rms_scale(hidden_perm, attn_gain_perm)
    qkv = jnp.dot(norm_in, qkv_full, preferred_element_type=jnp.float32).astype(jnp.bfloat16)
    queries = qkv[:, :q_cols]
    kv_part = qkv[:, q_cols:]
    kv_all = lax.all_to_all(
        jnp.broadcast_to(kv_part[None], (tp_size,) + kv_part.shape), "tp", 0, 0, tiled=True
    )
    per_dev = k_cols // KVH
    kv_index = tp_index * local_heads // (HEADS // KVH)

    def head_of(part):
        split = part.reshape(tp_size, row_count, per_dev, KVH)
        one = lax.dynamic_slice_in_dim(split, kv_index, 1, 3)[..., 0]
        return one.transpose(1, 0, 2).reshape(row_count, tp_size * per_dev)

    key_head = head_of(kv_all[:, :, :k_cols])
    value_head = head_of(kv_all[:, :, k_cols:])

    segs = segment_ids(lengths, block_rows)
    same = segs[:, :, None] == segs[:, None, :]
    blocked_queries = queries.reshape(blocks, block_rows, local_heads, HEAD_SIZE)
    blocked_keys = key_head.reshape(blocks, block_rows, HEAD_SIZE)
    blocked_values = value_head.reshape(blocks, block_rows, HEAD_SIZE)
    hidden_blocks = hidden_perm.reshape(blocks, block_rows, width)
    residual_parts, hidden_parts = [], []
    for b in range(blocks):
        attention_scores = jnp.einsum(
            "wre,pe->rwp", blocked_queries[b], blocked_keys[b], preferred_element_type=jnp.float32
        ) * HEAD_SIZE ** (-0.5)
        attention_scores = jnp.where(same[b][None, :, :], attention_scores, -1e30)
        attention_probabilities = softmax_rows(attention_scores)
        attended_rows = jnp.einsum(
            "sfo,on->fsn",
            attention_probabilities,
            blocked_values[b],
            preferred_element_type=jnp.float32,
        )
        attended_rows = attended_rows.astype(jnp.bfloat16).reshape(block_rows, local_heads * HEAD_SIZE)
        attn_term = transposed_dot(attended_rows, o_full).astype(jnp.bfloat16)
        if residual_parts:
            attn_term, _ = lax.optimization_barrier((attn_term, residual_parts[-1]))
        attn_total = lax.psum(attn_term, "tp").astype(jnp.float32)
        residual_b = hidden_blocks[b].astype(jnp.float32) + attn_total
        norm_mid = rms_scale(residual_b, ffn_gain_perm)
        gate_pre = jnp.dot(norm_mid, gate_full, preferred_element_type=jnp.float32)
        up_pre = jnp.dot(norm_mid, up_full, preferred_element_type=jnp.float32)
        hidden_parts.append((jax.nn.silu(gate_pre) * up_pre).astype(jnp.bfloat16))
        residual_parts.append(residual_b)
    residual = jnp.concatenate(residual_parts, 0)
    hidden_ffn = jnp.concatenate(hidden_parts, 0)

    block_index = lax.broadcasted_iota(jnp.int32, (blocks, block_rows), 0)
    program_of_row = (block_index * per_block + segs).reshape(row_count)
    program_grid = lax.broadcasted_iota(jnp.int32, (programs, row_count), 0)
    selector = (program_grid == program_of_row[None, :]).astype(jnp.float32)
    hidden_sums = jnp.dot(
        selector.astype(jnp.bfloat16), hidden_ffn, preferred_element_type=jnp.float32
    )
    chunk_owner = tp_index // ratio
    owner_step = jnp.argmax(order == chunk_owner).astype(jnp.int32)
    chunk_start = owner_step * d_grp + (tp_index % ratio) * d_tp
    residual_chunk = lax.dynamic_slice_in_dim(residual, chunk_start, d_tp, 1)
    residual_sums = jnp.dot(selector, residual_chunk, precision=HIGH, preferred_element_type=jnp.float32)

    hidden_all = gather_grp(hidden_sums, chips).reshape(grp_size * programs, -1)
    down_part = lax.dot_general(
        hidden_all, down_weight.astype(jnp.float32), (((1,), (1,)), ((), ())),
        precision=HIGH, preferred_element_type=jnp.float32,
    )

    dest_all = gather_grp(dest[:, 0], chips)
    lengths_all = gather_grp(lengths.reshape(programs), chips).reshape(grp_size * programs)
    grp_ids = lax.broadcasted_iota(jnp.int32, (grp_size, programs, grp_size), 2)
    chosen = (dest_all[:, :, None] == grp_ids).astype(jnp.int32)
    earlier = jnp.cumsum(chosen, axis=1) - chosen
    slot_rank = jnp.sum(earlier * chosen, axis=2)
    slot_row = order[:, None] * capacity + slot_rank
    slots = grp_size * capacity
    target_grid = lax.broadcasted_iota(jnp.int32, (grp_size, slots, grp_size, programs), 0)
    row_grid = lax.broadcasted_iota(jnp.int32, (grp_size, slots, grp_size, programs), 1)
    placer = (
        (target_grid == dest_all[None, None]) & (row_grid == slot_row[None, None])
    ).astype(jnp.float32).reshape(grp_size, slots, grp_size * programs)
    down_slots = jnp.einsum("asq,qd->asd", placer, down_part, precision=HIGH)
    down_slots = down_slots.reshape(grp_size, slots, ratio, d_tp).transpose(0, 2, 1, 3)
    send = lax.dynamic_update_slice(
        jnp.zeros((grp_size, tp_size, slots, d_tp), jnp.float32),
        down_slots,
        (0, grp_index * ratio, 0, 0),
    )
    local_placer = placer[:, :, :programs]
    residual_slots = jnp.einsum("asq,qd->asd", local_placer, residual_sums, precision=HIGH)
    send = send + lax.dynamic_update_slice(
        jnp.zeros((grp_size, tp_size, slots, d_tp), jnp.float32),
        residual_slots[:, None],
        (0, tp_index, 0, 0),
    )
    received = lax.all_to_all(
        send.reshape(grp_size * tp_size, slots, d_tp), ("grp", "tp"), 0, 0, tiled=True
    )
    totals = jnp.sum(received, axis=0)
    mine = lax.dynamic_index_in_dim(placer, grp_index, 0, keepdims=False)
    counts = jnp.dot(mine, lengths_all.astype(jnp.float32), precision=HIGH)
    counts = jnp.where(counts > 0, counts, 1.0)
    embedded = (totals / counts[:, None]).astype(jnp.bfloat16)
    return embedded.reshape(1, grp_size, capacity, d_tp)


def solution(mesh):
    placed = (
        P("grp", None),
        P("grp", None),
        P("grp", None),
        P(),
        P("grp", "tp"),
        P("grp", "tp"),
        P("grp", "tp"),
        P("grp", "tp"),
        P(),
        P("grp", "tp"),
        P("grp", "tp"),
        P("grp", "tp"),
    )
    return jax.shard_map(
        on_device, mesh=mesh, in_specs=placed, out_specs=P("grp", None, None, "tp"), check_vma=False
    )
```

```python
import jax
import jax.numpy as jnp
from jax import lax
from jax.sharding import PartitionSpec as P

HEAD_SIZE = 128
KVH = 4
HEADS = 16


EPSILON = 1e-06
HIGH = lax.Precision.HIGHEST


def rms_scale(rows, gain):
    rows = rows.astype(jnp.float32)
    factor = lax.rsqrt(jnp.mean(rows * rows, axis=1, keepdims=True) + EPSILON)
    return (rows * factor * gain[None, :]).astype(jnp.bfloat16)


def segment_ids(lengths, block_rows):
    bounds = jnp.cumsum(lengths, axis=1)
    position = lax.broadcasted_iota(jnp.int32, (lengths.shape[0], block_rows), 1)
    return jnp.sum((position[:, :, None] >= bounds[:, None, :]).astype(jnp.int32), axis=2)


def softmax_rows(attention_scores):
    top = jnp.max(attention_scores, axis=-1, keepdims=True)
    expo = jnp.exp(attention_scores - top)
    return (expo / jnp.sum(expo, axis=-1, keepdims=True)).astype(jnp.bfloat16)


def transposed_dot(left, right):
    return lax.dot_general(
        left, right, (((1,), (1,)), ((), ())), preferred_element_type=jnp.float32
    )


def gather_grp(piece, chips):
    held = [piece]
    moving = piece
    if chips > 1:
        ring = [(2 * i + c, 2 * ((i + 1) % chips) + c) for i in range(chips) for c in range(2)]
        for _ in range(chips - 1):
            moving = lax.ppermute(moving, "grp", ring)
            held.append(moving)
    mine = jnp.stack(held)
    other = lax.ppermute(mine, "grp", [(g, g ^ 1) for g in range(2 * chips)])
    return jnp.concatenate([mine, other], 0)


def source_order(chips):
    g = lax.axis_index("grp")
    chip, core = g // 2, g % 2
    steps = jnp.arange(chips, dtype=jnp.int32)
    own = 2 * ((chip - steps) % chips) + core
    return jnp.concatenate([own, own - core + (1 - core)])


def take_blocks(x, order, size, axis):
    return jnp.concatenate(
        [lax.dynamic_slice_in_dim(x, order[k] * size, size, axis) for k in range(order.shape[0])],
        axis,
    )


def ring_walk(n):
    if n % 2:
        return list(range(n))
    return list(range(0, n, 2)) + list(range(n - 1, 0, -2))


def ring_psum(x, axis, n):
    walk = ring_walk(n)
    place = [0] * n
    for p, t in enumerate(walk):
        place[t] = p
    pos = jnp.asarray(place, jnp.int32)[lax.axis_index(axis)]
    rows, half = x.shape[0], x.shape[1] // 2
    size = rows // n
    parts = []
    for sign, local in ((1, x[:, :half]), (-1, x[:, half:])):
        pairs = [(walk[p], walk[(p + sign) % n]) for p in range(n)]

        def chunk(k):
            return lax.dynamic_slice_in_dim(local, ((pos - sign * k) % n) * size, size, 0)

        acc = chunk(0)
        for step in range(n - 1):
            got = lax.ppermute(acc, axis, pairs)
            acc = (got.astype(jnp.float32) + chunk(step + 1).astype(jnp.float32)).astype(x.dtype)
        out = jnp.zeros_like(local)
        moving = acc
        for step in range(n):
            if step:
                moving = lax.ppermute(moving, axis, pairs)
            where = ((pos + sign - sign * step) % n) * size
            out = lax.dynamic_update_slice_in_dim(out, moving, where, 0)
        parts.append(out)
    return jnp.concatenate(parts, 1)


def on_device(
    hidden_in,
    lengths,
    dest,
    attn_gain,
    q_weight,
    k_weight,
    v_weight,
    o_weight,
    ffn_gain,
    gate_weight,
    up_weight,
    down_weight,
):
    row_count, width = hidden_in.shape
    blocks, per_block = lengths.shape
    block_rows = row_count // blocks
    programs = blocks * per_block
    tp_size = lax.axis_size("tp")
    grp_size = lax.axis_size("grp")
    chips = grp_size // 2
    tp_index = lax.axis_index("tp")
    grp_index = lax.axis_index("grp")
    d_grp = width // grp_size
    d_tp = width // tp_size
    ratio = tp_size // grp_size
    capacity = max(2, (programs + grp_size - 1) // grp_size)
    local_heads = q_weight.shape[1] // HEAD_SIZE
    order = source_order(chips)

    q_cols, k_cols = q_weight.shape[1], k_weight.shape[1]
    qkv_full = gather_grp(jnp.concatenate([q_weight, k_weight, v_weight], 1), chips)
    qkv_full = qkv_full.reshape(width, -1)
    o_after, qkv_full = lax.optimization_barrier((o_weight, qkv_full))
    o_full = gather_grp(o_after, chips).reshape(width, -1)
    gate_after, up_after, o_full = lax.optimization_barrier((gate_weight, up_weight, o_full))
    gate_full = gather_grp(gate_after, chips).reshape(width, -1)
    up_full = gather_grp(up_after, chips).reshape(width, -1)

    hidden_perm = take_blocks(hidden_in, order, d_grp, 1)
    attn_gain_perm = take_blocks(attn_gain, order, d_grp, 0)
    ffn_gain_perm = take_blocks(ffn_gain, order, d_grp, 0)

    norm_in = rms_scale(hidden_perm, attn_gain_perm)
    qkv = jnp.dot(norm_in, qkv_full, preferred_element_type=jnp.float32).astype(jnp.bfloat16)
    queries = qkv[:, :q_cols]
    kv_part = qkv[:, q_cols:]
    kv_all = lax.all_to_all(
        jnp.broadcast_to(kv_part[None], (tp_size,) + kv_part.shape), "tp", 0, 0, tiled=True
    )
    per_dev = k_cols // KVH
    kv_index = tp_index * local_heads // (HEADS // KVH)

    def head_of(part):
        split = part.reshape(tp_size, row_count, per_dev, KVH)
        one = lax.dynamic_slice_in_dim(split, kv_index, 1, 3)[..., 0]
        return one.transpose(1, 0, 2).reshape(row_count, tp_size * per_dev)

    key_head = head_of(kv_all[:, :, :k_cols])
    value_head = head_of(kv_all[:, :, k_cols:])

    segs = segment_ids(lengths, block_rows)
    same = segs[:, :, None] == segs[:, None, :]
    blocked_queries = queries.reshape(blocks, block_rows, local_heads, HEAD_SIZE)
    blocked_keys = key_head.reshape(blocks, block_rows, HEAD_SIZE)
    blocked_values = value_head.reshape(blocks, block_rows, HEAD_SIZE)
    attention_scores = jnp.einsum(
        "xwre,xpe->xrwp", blocked_queries, blocked_keys, preferred_element_type=jnp.float32
    ) * HEAD_SIZE ** (-0.5)
    attention_scores = jnp.where(same[:, None, :, :], attention_scores, -1e30)
    attention_probabilities = softmax_rows(attention_scores)
    attended_rows = jnp.einsum(
        "asfo,aon->afsn",
        attention_probabilities,
        blocked_values,
        preferred_element_type=jnp.float32,
    )
    attended_rows = attended_rows.astype(jnp.bfloat16).reshape(row_count, local_heads * HEAD_SIZE)
    attn_term = transposed_dot(attended_rows, o_full).astype(jnp.bfloat16)
    attn_total = ring_psum(attn_term, "tp", tp_size).astype(jnp.float32)
    residual = hidden_perm.astype(jnp.float32) + attn_total
    norm_mid = rms_scale(residual, ffn_gain_perm)
    gate_pre = jnp.dot(norm_mid, gate_full, preferred_element_type=jnp.float32)
    up_pre = jnp.dot(norm_mid, up_full, preferred_element_type=jnp.float32)
    hidden_ffn = (jax.nn.silu(gate_pre) * up_pre).astype(jnp.bfloat16)

    block_index = lax.broadcasted_iota(jnp.int32, (blocks, block_rows), 0)
    program_of_row = (block_index * per_block + segs).reshape(row_count)
    program_grid = lax.broadcasted_iota(jnp.int32, (programs, row_count), 0)
    selector = (program_grid == program_of_row[None, :]).astype(jnp.float32)
    hidden_sums = jnp.dot(
        selector.astype(jnp.bfloat16), hidden_ffn, preferred_element_type=jnp.float32
    )
    chunk_owner = tp_index // ratio
    owner_step = jnp.argmax(order == chunk_owner).astype(jnp.int32)
    chunk_start = owner_step * d_grp + (tp_index % ratio) * d_tp
    residual_chunk = lax.dynamic_slice_in_dim(residual, chunk_start, d_tp, 1)
    residual_sums = jnp.dot(selector, residual_chunk, precision=HIGH, preferred_element_type=jnp.float32)

    hidden_all = gather_grp(hidden_sums, chips).reshape(grp_size * programs, -1)
    down_part = lax.dot_general(
        hidden_all, down_weight.astype(jnp.float32), (((1,), (1,)), ((), ())),
        precision=HIGH, preferred_element_type=jnp.float32,
    )

    dest_all = gather_grp(dest[:, 0], chips)
    lengths_all = gather_grp(lengths.reshape(programs), chips).reshape(grp_size * programs)
    grp_ids = lax.broadcasted_iota(jnp.int32, (grp_size, programs, grp_size), 2)
    chosen = (dest_all[:, :, None] == grp_ids).astype(jnp.int32)
    earlier = jnp.cumsum(chosen, axis=1) - chosen
    slot_rank = jnp.sum(earlier * chosen, axis=2)
    slot_row = order[:, None] * capacity + slot_rank
    slots = grp_size * capacity
    target_grid = lax.broadcasted_iota(jnp.int32, (grp_size, slots, grp_size, programs), 0)
    row_grid = lax.broadcasted_iota(jnp.int32, (grp_size, slots, grp_size, programs), 1)
    placer = (
        (target_grid == dest_all[None, None]) & (row_grid == slot_row[None, None])
    ).astype(jnp.float32).reshape(grp_size, slots, grp_size * programs)
    down_slots = jnp.einsum("asq,qd->asd", placer, down_part, precision=HIGH)
    down_slots = down_slots.reshape(grp_size, slots, ratio, d_tp).transpose(0, 2, 1, 3)
    send = lax.dynamic_update_slice(
        jnp.zeros((grp_size, tp_size, slots, d_tp), jnp.float32),
        down_slots,
        (0, grp_index * ratio, 0, 0),
    )
    local_placer = placer[:, :, :programs]
    residual_slots = jnp.einsum("asq,qd->asd", local_placer, residual_sums, precision=HIGH)
    send = send + lax.dynamic_update_slice(
        jnp.zeros((grp_size, tp_size, slots, d_tp), jnp.float32),
        residual_slots[:, None],
        (0, tp_index, 0, 0),
    )
    received = lax.all_to_all(
        send.reshape(grp_size * tp_size, slots, d_tp), ("grp", "tp"), 0, 0, tiled=True
    )
    totals = jnp.sum(received, axis=0)
    mine = lax.dynamic_index_in_dim(placer, grp_index, 0, keepdims=False)
    counts = jnp.dot(mine, lengths_all.astype(jnp.float32), precision=HIGH)
    counts = jnp.where(counts > 0, counts, 1.0)
    embedded = (totals / counts[:, None]).astype(jnp.bfloat16)
    return embedded.reshape(1, grp_size, capacity, d_tp)


def solution(mesh):
    placed = (
        P("grp", None),
        P("grp", None),
        P("grp", None),
        P(),
        P("grp", "tp"),
        P("grp", "tp"),
        P("grp", "tp"),
        P("grp", "tp"),
        P(),
        P("grp", "tp"),
        P("grp", "tp"),
        P("grp", "tp"),
    )
    return jax.shard_map(
        on_device, mesh=mesh, in_specs=placed, out_specs=P("grp", None, None, "tp"), check_vma=False
    )
```

```python
import jax
import jax.numpy as jnp
from jax import lax
from jax.sharding import PartitionSpec as P

HEAD_SIZE = 128
KVH = 4
HEADS = 16


EPSILON = 1e-06
HIGH = lax.Precision.HIGHEST


def rms_scale(rows, gain):
    rows = rows.astype(jnp.float32)
    factor = lax.rsqrt(jnp.mean(rows * rows, axis=1, keepdims=True) + EPSILON)
    return (rows * factor * gain[None, :]).astype(jnp.bfloat16)


def segment_ids(lengths, block_rows):
    bounds = jnp.cumsum(lengths, axis=1)
    position = lax.broadcasted_iota(jnp.int32, (lengths.shape[0], block_rows), 1)
    return jnp.sum((position[:, :, None] >= bounds[:, None, :]).astype(jnp.int32), axis=2)


def softmax_rows(attention_scores):
    top = jnp.max(attention_scores, axis=-1, keepdims=True)
    expo = jnp.exp(attention_scores - top)
    return (expo / jnp.sum(expo, axis=-1, keepdims=True)).astype(jnp.bfloat16)


def transposed_dot(left, right):
    return lax.dot_general(
        left, right, (((1,), (1,)), ((), ())), preferred_element_type=jnp.float32
    )


def gather_grp(piece, chips):
    held = [piece]
    moving = piece
    if chips > 1:
        ring = [(2 * i + c, 2 * ((i + 1) % chips) + c) for i in range(chips) for c in range(2)]
        for _ in range(chips - 1):
            moving = lax.ppermute(moving, "grp", ring)
            held.append(moving)
    mine = jnp.stack(held)
    other = lax.ppermute(mine, "grp", [(g, g ^ 1) for g in range(2 * chips)])
    return jnp.concatenate([mine, other], 0)


def source_order(chips):
    g = lax.axis_index("grp")
    chip, core = g // 2, g % 2
    steps = jnp.arange(chips, dtype=jnp.int32)
    own = 2 * ((chip - steps) % chips) + core
    return jnp.concatenate([own, own - core + (1 - core)])


def take_blocks(x, order, size, axis):
    return jnp.concatenate(
        [lax.dynamic_slice_in_dim(x, order[k] * size, size, axis) for k in range(order.shape[0])],
        axis,
    )


def ring_walk(n):
    if n % 2:
        return list(range(n))
    return list(range(0, n, 2)) + list(range(n - 1, 0, -2))


def ring_psum(x, axis, n):
    walk = ring_walk(n)
    place = [0] * n
    for p, t in enumerate(walk):
        place[t] = p
    pos = jnp.asarray(place, jnp.int32)[lax.axis_index(axis)]
    rows, quarter = x.shape[0], x.shape[1] // 4
    size = rows // n
    parts = []
    for sign, local in (
        (1, x[:, :quarter]),
        (-1, x[:, quarter : 2 * quarter]),
        (1, x[:, 2 * quarter : 3 * quarter]),
        (-1, x[:, 3 * quarter :]),
    ):
        pairs = [(walk[p], walk[(p + sign) % n]) for p in range(n)]

        def chunk(k):
            return lax.dynamic_slice_in_dim(local, ((pos - sign * k) % n) * size, size, 0)

        acc = chunk(0)
        for step in range(n - 1):
            got = lax.ppermute(acc, axis, pairs)
            acc = (got.astype(jnp.float32) + chunk(step + 1).astype(jnp.float32)).astype(x.dtype)
        out = jnp.zeros_like(local)
        moving = acc
        for step in range(n):
            if step:
                moving = lax.ppermute(moving, axis, pairs)
            where = ((pos + sign - sign * step) % n) * size
            out = lax.dynamic_update_slice_in_dim(out, moving, where, 0)
        parts.append(out)
    return jnp.concatenate(parts, 1)


def on_device(
    hidden_in,
    lengths,
    dest,
    attn_gain,
    q_weight,
    k_weight,
    v_weight,
    o_weight,
    ffn_gain,
    gate_weight,
    up_weight,
    down_weight,
):
    row_count, width = hidden_in.shape
    blocks, per_block = lengths.shape
    block_rows = row_count // blocks
    programs = blocks * per_block
    tp_size = lax.axis_size("tp")
    grp_size = lax.axis_size("grp")
    chips = grp_size // 2
    tp_index = lax.axis_index("tp")
    grp_index = lax.axis_index("grp")
    d_grp = width // grp_size
    d_tp = width // tp_size
    ratio = tp_size // grp_size
    capacity = max(2, (programs + grp_size - 1) // grp_size)
    local_heads = q_weight.shape[1] // HEAD_SIZE
    order = source_order(chips)

    q_cols, k_cols = q_weight.shape[1], k_weight.shape[1]
    qkv_full = gather_grp(jnp.concatenate([q_weight, k_weight, v_weight], 1), chips)
    qkv_full = qkv_full.reshape(width, -1)
    o_after, qkv_full = lax.optimization_barrier((o_weight, qkv_full))
    o_full = gather_grp(o_after, chips).reshape(width, -1)
    gate_after, up_after, o_full = lax.optimization_barrier((gate_weight, up_weight, o_full))
    gate_full = gather_grp(gate_after, chips).reshape(width, -1)
    up_full = gather_grp(up_after, chips).reshape(width, -1)

    hidden_perm = take_blocks(hidden_in, order, d_grp, 1)
    attn_gain_perm = take_blocks(attn_gain, order, d_grp, 0)
    ffn_gain_perm = take_blocks(ffn_gain, order, d_grp, 0)

    norm_in = rms_scale(hidden_perm, attn_gain_perm)
    qkv = jnp.dot(norm_in, qkv_full, preferred_element_type=jnp.float32).astype(jnp.bfloat16)
    queries = qkv[:, :q_cols]
    kv_part = qkv[:, q_cols:]
    kv_all = lax.all_to_all(
        jnp.broadcast_to(kv_part[None], (tp_size,) + kv_part.shape), "tp", 0, 0, tiled=True
    )
    per_dev = k_cols // KVH
    kv_index = tp_index * local_heads // (HEADS // KVH)

    def head_of(part):
        split = part.reshape(tp_size, row_count, per_dev, KVH)
        one = lax.dynamic_slice_in_dim(split, kv_index, 1, 3)[..., 0]
        return one.transpose(1, 0, 2).reshape(row_count, tp_size * per_dev)

    key_head = head_of(kv_all[:, :, :k_cols])
    value_head = head_of(kv_all[:, :, k_cols:])

    segs = segment_ids(lengths, block_rows)
    same = segs[:, :, None] == segs[:, None, :]
    blocked_queries = queries.reshape(blocks, block_rows, local_heads, HEAD_SIZE)
    blocked_keys = key_head.reshape(blocks, block_rows, HEAD_SIZE)
    blocked_values = value_head.reshape(blocks, block_rows, HEAD_SIZE)
    attention_scores = jnp.einsum(
        "xwre,xpe->xrwp", blocked_queries, blocked_keys, preferred_element_type=jnp.float32
    ) * HEAD_SIZE ** (-0.5)
    attention_scores = jnp.where(same[:, None, :, :], attention_scores, -1e30)
    attention_probabilities = softmax_rows(attention_scores)
    attended_rows = jnp.einsum(
        "asfo,aon->afsn",
        attention_probabilities,
        blocked_values,
        preferred_element_type=jnp.float32,
    )
    attended_rows = attended_rows.astype(jnp.bfloat16).reshape(row_count, local_heads * HEAD_SIZE)
    attn_term = transposed_dot(attended_rows, o_full).astype(jnp.bfloat16)
    attn_total = ring_psum(attn_term, "tp", tp_size).astype(jnp.float32)
    residual = hidden_perm.astype(jnp.float32) + attn_total
    norm_mid = rms_scale(residual, ffn_gain_perm)
    gate_pre = jnp.dot(norm_mid, gate_full, preferred_element_type=jnp.float32)
    up_pre = jnp.dot(norm_mid, up_full, preferred_element_type=jnp.float32)
    hidden_ffn = (jax.nn.silu(gate_pre) * up_pre).astype(jnp.bfloat16)

    block_index = lax.broadcasted_iota(jnp.int32, (blocks, block_rows), 0)
    program_of_row = (block_index * per_block + segs).reshape(row_count)
    program_grid = lax.broadcasted_iota(jnp.int32, (programs, row_count), 0)
    selector = (program_grid == program_of_row[None, :]).astype(jnp.float32)
    hidden_sums = jnp.dot(
        selector.astype(jnp.bfloat16), hidden_ffn, preferred_element_type=jnp.float32
    )
    chunk_owner = tp_index // ratio
    owner_step = jnp.argmax(order == chunk_owner).astype(jnp.int32)
    chunk_start = owner_step * d_grp + (tp_index % ratio) * d_tp
    residual_chunk = lax.dynamic_slice_in_dim(residual, chunk_start, d_tp, 1)
    residual_sums = jnp.dot(selector, residual_chunk, precision=HIGH, preferred_element_type=jnp.float32)

    hidden_all = gather_grp(hidden_sums, chips).reshape(grp_size * programs, -1)
    down_part = lax.dot_general(
        hidden_all, down_weight.astype(jnp.float32), (((1,), (1,)), ((), ())),
        precision=HIGH, preferred_element_type=jnp.float32,
    )

    dest_all = gather_grp(dest[:, 0], chips)
    lengths_all = gather_grp(lengths.reshape(programs), chips).reshape(grp_size * programs)
    grp_ids = lax.broadcasted_iota(jnp.int32, (grp_size, programs, grp_size), 2)
    chosen = (dest_all[:, :, None] == grp_ids).astype(jnp.int32)
    earlier = jnp.cumsum(chosen, axis=1) - chosen
    slot_rank = jnp.sum(earlier * chosen, axis=2)
    slot_row = order[:, None] * capacity + slot_rank
    slots = grp_size * capacity
    target_grid = lax.broadcasted_iota(jnp.int32, (grp_size, slots, grp_size, programs), 0)
    row_grid = lax.broadcasted_iota(jnp.int32, (grp_size, slots, grp_size, programs), 1)
    placer = (
        (target_grid == dest_all[None, None]) & (row_grid == slot_row[None, None])
    ).astype(jnp.float32).reshape(grp_size, slots, grp_size * programs)
    down_slots = jnp.einsum("asq,qd->asd", placer, down_part, precision=HIGH)
    down_slots = down_slots.reshape(grp_size, slots, ratio, d_tp).transpose(0, 2, 1, 3)
    send = lax.dynamic_update_slice(
        jnp.zeros((grp_size, tp_size, slots, d_tp), jnp.float32),
        down_slots,
        (0, grp_index * ratio, 0, 0),
    )
    local_placer = placer[:, :, :programs]
    residual_slots = jnp.einsum("asq,qd->asd", local_placer, residual_sums, precision=HIGH)
    send = send + lax.dynamic_update_slice(
        jnp.zeros((grp_size, tp_size, slots, d_tp), jnp.float32),
        residual_slots[:, None],
        (0, tp_index, 0, 0),
    )
    received = lax.all_to_all(
        send.reshape(grp_size * tp_size, slots, d_tp), ("grp", "tp"), 0, 0, tiled=True
    )
    totals = jnp.sum(received, axis=0)
    mine = lax.dynamic_index_in_dim(placer, grp_index, 0, keepdims=False)
    counts = jnp.dot(mine, lengths_all.astype(jnp.float32), precision=HIGH)
    counts = jnp.where(counts > 0, counts, 1.0)
    embedded = (totals / counts[:, None]).astype(jnp.bfloat16)
    return embedded.reshape(1, grp_size, capacity, d_tp)


def solution(mesh):
    placed = (
        P("grp", None),
        P("grp", None),
        P("grp", None),
        P(),
        P("grp", "tp"),
        P("grp", "tp"),
        P("grp", "tp"),
        P("grp", "tp"),
        P(),
        P("grp", "tp"),
        P("grp", "tp"),
        P("grp", "tp"),
    )
    return jax.shard_map(
        on_device, mesh=mesh, in_specs=placed, out_specs=P("grp", None, None, "tp"), check_vma=False
    )
```

```python
import jax
import jax.numpy as jnp
from jax import lax
from jax.sharding import PartitionSpec as P

HEAD_SIZE = 128
KVH = 4
HEADS = 16


EPSILON = 1e-06
HIGH = lax.Precision.HIGHEST


def rms_scale(rows, gain):
    rows = rows.astype(jnp.float32)
    factor = lax.rsqrt(jnp.mean(rows * rows, axis=1, keepdims=True) + EPSILON)
    return (rows * factor * gain[None, :]).astype(jnp.bfloat16)


def segment_ids(lengths, block_rows):
    bounds = jnp.cumsum(lengths, axis=1)
    position = lax.broadcasted_iota(jnp.int32, (lengths.shape[0], block_rows), 1)
    return jnp.sum((position[:, :, None] >= bounds[:, None, :]).astype(jnp.int32), axis=2)


def softmax_rows(attention_scores):
    top = jnp.max(attention_scores, axis=-1, keepdims=True)
    expo = jnp.exp(attention_scores - top)
    return (expo / jnp.sum(expo, axis=-1, keepdims=True)).astype(jnp.bfloat16)


def transposed_dot(left, right):
    return lax.dot_general(
        left, right, (((1,), (1,)), ((), ())), preferred_element_type=jnp.float32
    )


def gather_grp(piece, chips):
    held = [piece]
    moving = piece
    if chips > 1:
        ring = [(2 * i + c, 2 * ((i + 1) % chips) + c) for i in range(chips) for c in range(2)]
        for _ in range(chips - 1):
            moving = lax.ppermute(moving, "grp", ring)
            held.append(moving)
    mine = jnp.stack(held)
    other = lax.ppermute(mine, "grp", [(g, g ^ 1) for g in range(2 * chips)])
    return jnp.concatenate([mine, other], 0)


def source_order(chips):
    g = lax.axis_index("grp")
    chip, core = g // 2, g % 2
    steps = jnp.arange(chips, dtype=jnp.int32)
    own = 2 * ((chip - steps) % chips) + core
    return jnp.concatenate([own, own - core + (1 - core)])


def take_blocks(x, order, size, axis):
    return jnp.concatenate(
        [lax.dynamic_slice_in_dim(x, order[k] * size, size, axis) for k in range(order.shape[0])],
        axis,
    )


def ring_walk(n):
    if n % 2:
        return list(range(n))
    return list(range(0, n, 2)) + list(range(n - 1, 0, -2))


def ring_psum(x, axis, n):
    walk = ring_walk(n)
    place = [0] * n
    for p, t in enumerate(walk):
        place[t] = p
    pos = jnp.asarray(place, jnp.int32)[lax.axis_index(axis)]
    rows, half = x.shape[0], x.shape[1] // 2
    size = rows // n
    parts = []
    for sign, local in ((1, x[:, :half]), (-1, x[:, half:])):
        pairs = [(walk[p], walk[(p + sign) % n]) for p in range(n)]

        def chunk(k):
            return lax.dynamic_slice_in_dim(local, ((pos - sign * k) % n) * size, size, 0)

        acc = chunk(0)
        for step in range(n - 1):
            got = lax.ppermute(acc, axis, pairs)
            acc = (got.astype(jnp.float32) + chunk(step + 1).astype(jnp.float32)).astype(x.dtype)
        out = jnp.zeros_like(local)
        moving = acc
        for step in range(n):
            if step:
                moving = lax.ppermute(moving, axis, pairs)
            where = ((pos + sign - sign * step) % n) * size
            out = lax.dynamic_update_slice_in_dim(out, moving, where, 0)
        parts.append(out)
    return jnp.concatenate(parts, 1)


def on_device(
    hidden_in,
    lengths,
    dest,
    attn_gain,
    q_weight,
    k_weight,
    v_weight,
    o_weight,
    ffn_gain,
    gate_weight,
    up_weight,
    down_weight,
):
    row_count, width = hidden_in.shape
    blocks, per_block = lengths.shape
    block_rows = row_count // blocks
    programs = blocks * per_block
    tp_size = lax.axis_size("tp")
    grp_size = lax.axis_size("grp")
    chips = grp_size // 2
    tp_index = lax.axis_index("tp")
    grp_index = lax.axis_index("grp")
    d_grp = width // grp_size
    d_tp = width // tp_size
    ratio = tp_size // grp_size
    capacity = max(2, (programs + grp_size - 1) // grp_size)
    local_heads = q_weight.shape[1] // HEAD_SIZE
    order = source_order(chips)

    q_cols, k_cols = q_weight.shape[1], k_weight.shape[1]
    qkv_full = gather_grp(jnp.concatenate([q_weight, k_weight, v_weight], 1), chips)
    qkv_full = qkv_full.reshape(width, -1)
    o_after, qkv_full = lax.optimization_barrier((o_weight, qkv_full))
    o_full = gather_grp(o_after, chips).reshape(width, -1)
    gate_after, up_after, o_full = lax.optimization_barrier((gate_weight, up_weight, o_full))
    gate_full = gather_grp(gate_after, chips).reshape(width, -1)
    up_full = gather_grp(up_after, chips).reshape(width, -1)

    hidden_perm = take_blocks(hidden_in, order, d_grp, 1)
    attn_gain_perm = take_blocks(attn_gain, order, d_grp, 0)
    ffn_gain_perm = take_blocks(ffn_gain, order, d_grp, 0)

    norm_in = rms_scale(hidden_perm, attn_gain_perm)
    qkv = jnp.dot(norm_in, qkv_full, preferred_element_type=jnp.float32).astype(jnp.bfloat16)
    queries = qkv[:, :q_cols]
    per_dev = k_cols // KVH
    group_heads = HEADS // KVH
    key_split = qkv[:, q_cols : q_cols + k_cols].reshape(row_count, per_dev, KVH)
    value_split = qkv[:, q_cols + k_cols :].reshape(row_count, per_dev, KVH)
    outgoing_kv = jnp.stack(
        [
            jnp.concatenate(
                [key_split[:, :, u * local_heads // group_heads], value_split[:, :, u * local_heads // group_heads]],
                1,
            )
            for u in range(tp_size)
        ]
    )
    kv_in = lax.all_to_all(outgoing_kv, "tp", 0, 0, tiled=True)
    key_head = kv_in[:, :, :per_dev].transpose(1, 0, 2).reshape(row_count, tp_size * per_dev)
    value_head = kv_in[:, :, per_dev:].transpose(1, 0, 2).reshape(row_count, tp_size * per_dev)

    segs = segment_ids(lengths, block_rows)
    same = segs[:, :, None] == segs[:, None, :]
    blocked_queries = queries.reshape(blocks, block_rows, local_heads, HEAD_SIZE)
    blocked_keys = key_head.reshape(blocks, block_rows, HEAD_SIZE)
    blocked_values = value_head.reshape(blocks, block_rows, HEAD_SIZE)
    attention_scores = jnp.einsum(
        "xwre,xpe->xrwp", blocked_queries, blocked_keys, preferred_element_type=jnp.float32
    ) * HEAD_SIZE ** (-0.5)
    attention_scores = jnp.where(same[:, None, :, :], attention_scores, -1e30)
    attention_probabilities = softmax_rows(attention_scores)
    attended_rows = jnp.einsum(
        "asfo,aon->afsn",
        attention_probabilities,
        blocked_values,
        preferred_element_type=jnp.float32,
    )
    attended_rows = attended_rows.astype(jnp.bfloat16).reshape(row_count, local_heads * HEAD_SIZE)
    attn_term = transposed_dot(attended_rows, o_full).astype(jnp.bfloat16)
    attn_total = ring_psum(attn_term, "tp", tp_size).astype(jnp.float32)
    residual = hidden_perm.astype(jnp.float32) + attn_total
    norm_mid = rms_scale(residual, ffn_gain_perm)
    gate_pre = jnp.dot(norm_mid, gate_full, preferred_element_type=jnp.float32)
    up_pre = jnp.dot(norm_mid, up_full, preferred_element_type=jnp.float32)
    hidden_ffn = (jax.nn.silu(gate_pre) * up_pre).astype(jnp.bfloat16)

    block_index = lax.broadcasted_iota(jnp.int32, (blocks, block_rows), 0)
    program_of_row = (block_index * per_block + segs).reshape(row_count)
    program_grid = lax.broadcasted_iota(jnp.int32, (programs, row_count), 0)
    selector = (program_grid == program_of_row[None, :]).astype(jnp.float32)
    hidden_sums = jnp.dot(
        selector.astype(jnp.bfloat16), hidden_ffn, preferred_element_type=jnp.float32
    )
    chunk_owner = tp_index // ratio
    owner_step = jnp.argmax(order == chunk_owner).astype(jnp.int32)
    chunk_start = owner_step * d_grp + (tp_index % ratio) * d_tp
    residual_chunk = lax.dynamic_slice_in_dim(residual, chunk_start, d_tp, 1)
    residual_sums = jnp.dot(selector, residual_chunk, precision=HIGH, preferred_element_type=jnp.float32)

    hidden_all = gather_grp(hidden_sums, chips).reshape(grp_size * programs, -1)
    down_part = lax.dot_general(
        hidden_all, down_weight.astype(jnp.float32), (((1,), (1,)), ((), ())),
        precision=HIGH, preferred_element_type=jnp.float32,
    )

    dest_all = gather_grp(dest[:, 0], chips)
    lengths_all = gather_grp(lengths.reshape(programs), chips).reshape(grp_size * programs)
    grp_ids = lax.broadcasted_iota(jnp.int32, (grp_size, programs, grp_size), 2)
    chosen = (dest_all[:, :, None] == grp_ids).astype(jnp.int32)
    earlier = jnp.cumsum(chosen, axis=1) - chosen
    slot_rank = jnp.sum(earlier * chosen, axis=2)
    slot_row = order[:, None] * capacity + slot_rank
    slots = grp_size * capacity
    target_grid = lax.broadcasted_iota(jnp.int32, (grp_size, slots, grp_size, programs), 0)
    row_grid = lax.broadcasted_iota(jnp.int32, (grp_size, slots, grp_size, programs), 1)
    placer = (
        (target_grid == dest_all[None, None]) & (row_grid == slot_row[None, None])
    ).astype(jnp.float32).reshape(grp_size, slots, grp_size * programs)
    down_slots = jnp.einsum("asq,qd->asd", placer, down_part, precision=HIGH)
    totals = jnp.zeros((slots, d_tp), jnp.float32)
    for k in range(tp_size):
        pairs = []
        for g in range(grp_size):
            for t in range(tp_size):
                u = (t - k) % tp_size
                pairs.append((g * tp_size + t, (u // ratio) * tp_size + g * ratio + u % ratio))
        u = (tp_index - k) % tp_size
        piece = lax.dynamic_index_in_dim(down_slots, u // ratio, 0, keepdims=False)
        piece = lax.dynamic_slice_in_dim(piece, (u % ratio) * d_tp, d_tp, 1)
        totals = totals + lax.ppermute(piece, ("grp", "tp"), pairs)
    local_placer = placer[:, :, :programs]
    own_rows = lax.dynamic_slice_in_dim(local_placer, grp_index * capacity, capacity, 1)
    residual_slots = jnp.einsum("asq,qd->asd", own_rows, residual_sums, precision=HIGH)
    residual_in = lax.all_to_all(residual_slots, "grp", 0, 0, tiled=True)
    totals = totals + residual_in.reshape(slots, d_tp)
    mine = lax.dynamic_index_in_dim(placer, grp_index, 0, keepdims=False)
    counts = jnp.dot(mine, lengths_all.astype(jnp.float32), precision=HIGH)
    counts = jnp.where(counts > 0, counts, 1.0)
    embedded = (totals / counts[:, None]).astype(jnp.bfloat16)
    return embedded.reshape(1, grp_size, capacity, d_tp)


def solution(mesh):
    placed = (
        P("grp", None),
        P("grp", None),
        P("grp", None),
        P(),
        P("grp", "tp"),
        P("grp", "tp"),
        P("grp", "tp"),
        P("grp", "tp"),
        P(),
        P("grp", "tp"),
        P("grp", "tp"),
        P("grp", "tp"),
    )
    return jax.shard_map(
        on_device, mesh=mesh, in_specs=placed, out_specs=P("grp", None, None, "tp"), check_vma=False
    )
```

```python
import jax
import jax.numpy as jnp
from jax import lax
from jax.sharding import PartitionSpec as P

HEAD_SIZE = 128
KVH = 4
HEADS = 16


EPSILON = 1e-06
HIGH = lax.Precision.HIGHEST


def rms_scale(rows, gain):
    rows = rows.astype(jnp.float32)
    factor = lax.rsqrt(jnp.mean(rows * rows, axis=1, keepdims=True) + EPSILON)
    return (rows * factor * gain[None, :]).astype(jnp.bfloat16)


def segment_ids(lengths, block_rows):
    bounds = jnp.cumsum(lengths, axis=1)
    position = lax.broadcasted_iota(jnp.int32, (lengths.shape[0], block_rows), 1)
    return jnp.sum((position[:, :, None] >= bounds[:, None, :]).astype(jnp.int32), axis=2)


def softmax_rows(attention_scores):
    top = jnp.max(attention_scores, axis=-1, keepdims=True)
    expo = jnp.exp(attention_scores - top)
    return (expo / jnp.sum(expo, axis=-1, keepdims=True)).astype(jnp.bfloat16)


def transposed_dot(left, right):
    return lax.dot_general(
        left, right, (((1,), (1,)), ((), ())), preferred_element_type=jnp.float32
    )


def gather_chips(piece, chips):
    held = [piece]
    moving = piece
    if chips > 1:
        ring = [(2 * i + c, 2 * ((i + 1) % chips) + c) for i in range(chips) for c in range(2)]
        for _ in range(chips - 1):
            moving = lax.ppermute(moving, "grp", ring)
            held.append(moving)
    return jnp.stack(held)


def gather_cores(mine, chips):
    other = lax.ppermute(mine, "grp", [(g, g ^ 1) for g in range(2 * chips)])
    return jnp.concatenate([mine, other], 0)


def gather_grp(piece, chips):
    return gather_cores(gather_chips(piece, chips), chips)


def source_order(chips):
    g = lax.axis_index("grp")
    chip, core = g // 2, g % 2
    steps = jnp.arange(chips, dtype=jnp.int32)
    own = 2 * ((chip - steps) % chips) + core
    return jnp.concatenate([own, own - core + (1 - core)])


def take_blocks(x, order, size, axis):
    return jnp.concatenate(
        [lax.dynamic_slice_in_dim(x, order[k] * size, size, axis) for k in range(order.shape[0])],
        axis,
    )


def ring_walk(n):
    if n % 2:
        return list(range(n))
    return list(range(0, n, 2)) + list(range(n - 1, 0, -2))


def ring_psum(x, axis, n, ride):
    walk = ring_walk(n)
    place = [0] * n
    for p, t in enumerate(walk):
        place[t] = p
    pos = jnp.asarray(place, jnp.int32)[lax.axis_index(axis)]
    rows, half = x.shape[0], x.shape[1] // 2
    size = rows // n
    parts = []
    for sign, local in ((1, x[:, :half]), (-1, x[:, half:])):
        pairs = [(walk[p], walk[(p + sign) % n]) for p in range(n)]

        def chunk(k):
            return lax.dynamic_slice_in_dim(local, ((pos - sign * k) % n) * size, size, 0)

        acc = chunk(0)
        for step in range(n - 1):
            got = lax.ppermute(acc, axis, pairs)
            acc = (got.astype(jnp.float32) + chunk(step + 1).astype(jnp.float32)).astype(x.dtype)
        out = jnp.zeros_like(local)
        moving = acc
        for step in range(n):
            if step:
                moving = lax.ppermute(moving, axis, pairs)
            if step == min(2, n - 1) and sign == 1:
                moving, ride = lax.optimization_barrier((moving, ride))
            where = ((pos + sign - sign * step) % n) * size
            out = lax.dynamic_update_slice_in_dim(out, moving, where, 0)
        parts.append(out)
    return jnp.concatenate(parts, 1), ride


def on_device(
    hidden_in,
    lengths,
    dest,
    attn_gain,
    q_weight,
    k_weight,
    v_weight,
    o_weight,
    ffn_gain,
    gate_weight,
    up_weight,
    down_weight,
):
    row_count, width = hidden_in.shape
    blocks, per_block = lengths.shape
    block_rows = row_count // blocks
    programs = blocks * per_block
    tp_size = lax.axis_size("tp")
    grp_size = lax.axis_size("grp")
    chips = grp_size // 2
    tp_index = lax.axis_index("tp")
    grp_index = lax.axis_index("grp")
    d_grp = width // grp_size
    d_tp = width // tp_size
    ratio = tp_size // grp_size
    capacity = max(2, (programs + grp_size - 1) // grp_size)
    local_heads = q_weight.shape[1] // HEAD_SIZE
    order = source_order(chips)

    q_cols, k_cols = q_weight.shape[1], k_weight.shape[1]
    qkv_full = gather_grp(jnp.concatenate([q_weight, k_weight, v_weight], 1), chips)
    qkv_full = qkv_full.reshape(width, -1)
    o_after, qkv_full = lax.optimization_barrier((o_weight, qkv_full))
    o_full = gather_grp(o_after, chips).reshape(width, -1)
    gate_after, up_after, o_full = lax.optimization_barrier((gate_weight, up_weight, o_full))
    gate_chips = gather_chips(gate_after, chips)
    up_chips = gather_chips(up_after, chips)

    hidden_perm = take_blocks(hidden_in, order, d_grp, 1)
    attn_gain_perm = take_blocks(attn_gain, order, d_grp, 0)
    ffn_gain_perm = take_blocks(ffn_gain, order, d_grp, 0)

    norm_in = rms_scale(hidden_perm, attn_gain_perm)
    qkv = jnp.dot(norm_in, qkv_full, preferred_element_type=jnp.float32).astype(jnp.bfloat16)
    queries = qkv[:, :q_cols]
    per_dev = k_cols // KVH
    group_heads = HEADS // KVH
    key_split = qkv[:, q_cols : q_cols + k_cols].reshape(row_count, per_dev, KVH)
    value_split = qkv[:, q_cols + k_cols :].reshape(row_count, per_dev, KVH)
    outgoing_kv = jnp.stack(
        [
            jnp.concatenate(
                [key_split[:, :, u * local_heads // group_heads], value_split[:, :, u * local_heads // group_heads]],
                1,
            )
            for u in range(tp_size)
        ]
    )
    kv_in = lax.all_to_all(outgoing_kv, "tp", 0, 0, tiled=True)
    key_head = kv_in[:, :, :per_dev].transpose(1, 0, 2).reshape(row_count, tp_size * per_dev)
    value_head = kv_in[:, :, per_dev:].transpose(1, 0, 2).reshape(row_count, tp_size * per_dev)

    segs = segment_ids(lengths, block_rows)
    same = segs[:, :, None] == segs[:, None, :]
    blocked_queries = queries.reshape(blocks, block_rows, local_heads, HEAD_SIZE)
    blocked_keys = key_head.reshape(blocks, block_rows, HEAD_SIZE)
    blocked_values = value_head.reshape(blocks, block_rows, HEAD_SIZE)
    attention_scores = jnp.einsum(
        "xwre,xpe->xrwp", blocked_queries, blocked_keys, preferred_element_type=jnp.float32
    ) * HEAD_SIZE ** (-0.5)
    attention_scores = jnp.where(same[:, None, :, :], attention_scores, -1e30)
    attention_probabilities = softmax_rows(attention_scores)
    attended_rows = jnp.einsum(
        "asfo,aon->afsn",
        attention_probabilities,
        blocked_values,
        preferred_element_type=jnp.float32,
    )
    attended_rows = attended_rows.astype(jnp.bfloat16).reshape(row_count, local_heads * HEAD_SIZE)
    attn_term = transposed_dot(attended_rows, o_full).astype(jnp.bfloat16)
    attn_total, (gate_chips, up_chips) = ring_psum(attn_term, "tp", tp_size, (gate_chips, up_chips))
    attn_total = attn_total.astype(jnp.float32)
    gate_full = gather_cores(gate_chips, chips).reshape(width, -1)
    up_full = gather_cores(up_chips, chips).reshape(width, -1)
    residual = hidden_perm.astype(jnp.float32) + attn_total
    norm_mid = rms_scale(residual, ffn_gain_perm)
    gate_pre = jnp.dot(norm_mid, gate_full, preferred_element_type=jnp.float32)
    up_pre = jnp.dot(norm_mid, up_full, preferred_element_type=jnp.float32)
    hidden_ffn = (jax.nn.silu(gate_pre) * up_pre).astype(jnp.bfloat16)

    block_index = lax.broadcasted_iota(jnp.int32, (blocks, block_rows), 0)
    program_of_row = (block_index * per_block + segs).reshape(row_count)
    program_grid = lax.broadcasted_iota(jnp.int32, (programs, row_count), 0)
    selector = (program_grid == program_of_row[None, :]).astype(jnp.float32)
    hidden_sums = jnp.dot(
        selector.astype(jnp.bfloat16), hidden_ffn, preferred_element_type=jnp.float32
    )
    chunk_owner = tp_index // ratio
    owner_step = jnp.argmax(order == chunk_owner).astype(jnp.int32)
    chunk_start = owner_step * d_grp + (tp_index % ratio) * d_tp
    residual_chunk = lax.dynamic_slice_in_dim(residual, chunk_start, d_tp, 1)
    residual_sums = jnp.dot(selector, residual_chunk, precision=HIGH, preferred_element_type=jnp.float32)

    hidden_all = gather_grp(hidden_sums, chips).reshape(grp_size * programs, -1)
    down_part = lax.dot_general(
        hidden_all, down_weight.astype(jnp.float32), (((1,), (1,)), ((), ())),
        precision=HIGH, preferred_element_type=jnp.float32,
    )

    dest_all = gather_grp(dest[:, 0], chips)
    lengths_all = gather_grp(lengths.reshape(programs), chips).reshape(grp_size * programs)
    grp_ids = lax.broadcasted_iota(jnp.int32, (grp_size, programs, grp_size), 2)
    chosen = (dest_all[:, :, None] == grp_ids).astype(jnp.int32)
    earlier = jnp.cumsum(chosen, axis=1) - chosen
    slot_rank = jnp.sum(earlier * chosen, axis=2)
    slot_row = order[:, None] * capacity + slot_rank
    slots = grp_size * capacity
    target_grid = lax.broadcasted_iota(jnp.int32, (grp_size, slots, grp_size, programs), 0)
    row_grid = lax.broadcasted_iota(jnp.int32, (grp_size, slots, grp_size, programs), 1)
    placer = (
        (target_grid == dest_all[None, None]) & (row_grid == slot_row[None, None])
    ).astype(jnp.float32).reshape(grp_size, slots, grp_size * programs)
    down_slots = jnp.einsum("asq,qd->asd", placer, down_part, precision=HIGH)
    totals = jnp.zeros((slots, d_tp), jnp.float32)
    for k in range(tp_size):
        pairs = []
        for g in range(grp_size):
            for t in range(tp_size):
                u = (t - k) % tp_size
                pairs.append((g * tp_size + t, (u // ratio) * tp_size + g * ratio + u % ratio))
        u = (tp_index - k) % tp_size
        piece = lax.dynamic_index_in_dim(down_slots, u // ratio, 0, keepdims=False)
        piece = lax.dynamic_slice_in_dim(piece, (u % ratio) * d_tp, d_tp, 1)
        totals = totals + lax.ppermute(piece, ("grp", "tp"), pairs)
    local_placer = placer[:, :, :programs]
    own_rows = lax.dynamic_slice_in_dim(local_placer, grp_index * capacity, capacity, 1)
    residual_slots = jnp.einsum("asq,qd->asd", own_rows, residual_sums, precision=HIGH)
    residual_in = lax.all_to_all(residual_slots, "grp", 0, 0, tiled=True)
    totals = totals + residual_in.reshape(slots, d_tp)
    mine = lax.dynamic_index_in_dim(placer, grp_index, 0, keepdims=False)
    counts = jnp.dot(mine, lengths_all.astype(jnp.float32), precision=HIGH)
    counts = jnp.where(counts > 0, counts, 1.0)
    embedded = (totals / counts[:, None]).astype(jnp.bfloat16)
    return embedded.reshape(1, grp_size, capacity, d_tp)


def solution(mesh):
    placed = (
        P("grp", None),
        P("grp", None),
        P("grp", None),
        P(),
        P("grp", "tp"),
        P("grp", "tp"),
        P("grp", "tp"),
        P("grp", "tp"),
        P(),
        P("grp", "tp"),
        P("grp", "tp"),
        P("grp", "tp"),
    )
    return jax.shard_map(
        on_device, mesh=mesh, in_specs=placed, out_specs=P("grp", None, None, "tp"), check_vma=False
    )
```

```python
import jax
import jax.numpy as jnp
from jax import lax
from jax.sharding import PartitionSpec as P

HEAD_SIZE = 128
KVH = 4
HEADS = 16


EPSILON = 1e-06
HIGH = lax.Precision.HIGHEST


def rms_scale(rows, gain):
    rows = rows.astype(jnp.float32)
    factor = lax.rsqrt(jnp.mean(rows * rows, axis=1, keepdims=True) + EPSILON)
    return (rows * factor * gain[None, :]).astype(jnp.bfloat16)


def segment_ids(lengths, block_rows):
    bounds = jnp.cumsum(lengths, axis=1)
    position = lax.broadcasted_iota(jnp.int32, (lengths.shape[0], block_rows), 1)
    return jnp.sum((position[:, :, None] >= bounds[:, None, :]).astype(jnp.int32), axis=2)


def softmax_rows(attention_scores):
    top = jnp.max(attention_scores, axis=-1, keepdims=True)
    expo = jnp.exp(attention_scores - top)
    return (expo / jnp.sum(expo, axis=-1, keepdims=True)).astype(jnp.bfloat16)


def transposed_dot(left, right):
    return lax.dot_general(
        left, right, (((1,), (1,)), ((), ())), preferred_element_type=jnp.float32
    )


def gather_chips(piece, chips):
    held = [piece]
    moving = piece
    if chips > 1:
        ring = [(2 * i + c, 2 * ((i + 1) % chips) + c) for i in range(chips) for c in range(2)]
        for _ in range(chips - 1):
            moving = lax.ppermute(moving, "grp", ring)
            held.append(moving)
    return jnp.stack(held)


def gather_cores(mine, chips):
    other = lax.ppermute(mine, "grp", [(g, g ^ 1) for g in range(2 * chips)])
    return jnp.concatenate([mine, other], 0)


def gather_grp(piece, chips):
    return gather_cores(gather_chips(piece, chips), chips)


def source_order(chips):
    g = lax.axis_index("grp")
    chip, core = g // 2, g % 2
    steps = jnp.arange(chips, dtype=jnp.int32)
    own = 2 * ((chip - steps) % chips) + core
    return jnp.concatenate([own, own - core + (1 - core)])


def take_blocks(x, order, size, axis):
    return jnp.concatenate(
        [lax.dynamic_slice_in_dim(x, order[k] * size, size, axis) for k in range(order.shape[0])],
        axis,
    )


def ring_walk(n):
    if n % 2:
        return list(range(n))
    return list(range(0, n, 2)) + list(range(n - 1, 0, -2))


def ring_psum(x, axis, n, ride, finish):
    walk = ring_walk(n)
    place = [0] * n
    for p, t in enumerate(walk):
        place[t] = p
    pos = jnp.asarray(place, jnp.int32)[lax.axis_index(axis)]
    rows, half = x.shape[0], x.shape[1] // 2
    size = rows // n
    parts = []
    for sign, local in ((1, x[:, :half]), (-1, x[:, half:])):
        pairs = [(walk[p], walk[(p + sign) % n]) for p in range(n)]

        def chunk(k):
            return lax.dynamic_slice_in_dim(local, ((pos - sign * k) % n) * size, size, 0)

        acc = chunk(0)
        for step in range(n - 1):
            got = lax.ppermute(acc, axis, pairs)
            acc = (got.astype(jnp.float32) + chunk(step + 1).astype(jnp.float32)).astype(x.dtype)
        out = jnp.zeros_like(local)
        moving = acc
        for step in range(n):
            if step:
                moving = lax.ppermute(moving, axis, pairs)
            if step == min(2, n - 1) and sign == 1:
                moving, ride = lax.optimization_barrier((moving, ride))
                ride = finish(ride)
            if step == n - 1 and sign == 1:
                moving, ride = lax.optimization_barrier((moving, ride))
            where = ((pos + sign - sign * step) % n) * size
            out = lax.dynamic_update_slice_in_dim(out, moving, where, 0)
        parts.append(out)
    return jnp.concatenate(parts, 1), ride


def on_device(
    hidden_in,
    lengths,
    dest,
    attn_gain,
    q_weight,
    k_weight,
    v_weight,
    o_weight,
    ffn_gain,
    gate_weight,
    up_weight,
    down_weight,
):
    row_count, width = hidden_in.shape
    blocks, per_block = lengths.shape
    block_rows = row_count // blocks
    programs = blocks * per_block
    tp_size = lax.axis_size("tp")
    grp_size = lax.axis_size("grp")
    chips = grp_size // 2
    tp_index = lax.axis_index("tp")
    grp_index = lax.axis_index("grp")
    d_grp = width // grp_size
    d_tp = width // tp_size
    ratio = tp_size // grp_size
    capacity = max(2, (programs + grp_size - 1) // grp_size)
    local_heads = q_weight.shape[1] // HEAD_SIZE
    order = source_order(chips)

    q_cols, k_cols = q_weight.shape[1], k_weight.shape[1]
    qkv_full = gather_grp(jnp.concatenate([q_weight, k_weight, v_weight], 1), chips)
    qkv_full = qkv_full.reshape(width, -1)
    o_after, qkv_full = lax.optimization_barrier((o_weight, qkv_full))
    o_full = gather_grp(o_after, chips).reshape(width, -1)
    gate_after, up_after, o_full = lax.optimization_barrier((gate_weight, up_weight, o_full))
    gate_chips = gather_chips(gate_after, chips)
    up_chips = gather_chips(up_after, chips)

    hidden_perm = take_blocks(hidden_in, order, d_grp, 1)
    attn_gain_perm = take_blocks(attn_gain, order, d_grp, 0)
    ffn_gain_perm = take_blocks(ffn_gain, order, d_grp, 0)

    norm_in = rms_scale(hidden_perm, attn_gain_perm)
    qkv = jnp.dot(norm_in, qkv_full, preferred_element_type=jnp.float32).astype(jnp.bfloat16)
    queries = qkv[:, :q_cols]
    per_dev = k_cols // KVH
    group_heads = HEADS // KVH
    key_split = qkv[:, q_cols : q_cols + k_cols].reshape(row_count, per_dev, KVH)
    value_split = qkv[:, q_cols + k_cols :].reshape(row_count, per_dev, KVH)
    outgoing_kv = jnp.stack(
        [
            jnp.concatenate(
                [key_split[:, :, u * local_heads // group_heads], value_split[:, :, u * local_heads // group_heads]],
                1,
            )
            for u in range(tp_size)
        ]
    )
    kv_in = lax.all_to_all(outgoing_kv, "tp", 0, 0, tiled=True)
    key_head = kv_in[:, :, :per_dev].transpose(1, 0, 2).reshape(row_count, tp_size * per_dev)
    value_head = kv_in[:, :, per_dev:].transpose(1, 0, 2).reshape(row_count, tp_size * per_dev)

    segs = segment_ids(lengths, block_rows)
    same = segs[:, :, None] == segs[:, None, :]
    blocked_queries = queries.reshape(blocks, block_rows, local_heads, HEAD_SIZE)
    blocked_keys = key_head.reshape(blocks, block_rows, HEAD_SIZE)
    blocked_values = value_head.reshape(blocks, block_rows, HEAD_SIZE)
    attention_scores = jnp.einsum(
        "xwre,xpe->xrwp", blocked_queries, blocked_keys, preferred_element_type=jnp.float32
    ) * HEAD_SIZE ** (-0.5)
    attention_scores = jnp.where(same[:, None, :, :], attention_scores, -1e30)
    attention_probabilities = softmax_rows(attention_scores)
    attended_rows = jnp.einsum(
        "asfo,aon->afsn",
        attention_probabilities,
        blocked_values,
        preferred_element_type=jnp.float32,
    )
    attended_rows = attended_rows.astype(jnp.bfloat16).reshape(row_count, local_heads * HEAD_SIZE)
    attn_term = transposed_dot(attended_rows, o_full).astype(jnp.bfloat16)
    attn_total, (gate_full, up_full) = ring_psum(
        attn_term,
        "tp",
        tp_size,
        (gate_chips, up_chips),
        lambda ride: tuple(gather_cores(w, chips).reshape(width, -1) for w in ride),
    )
    attn_total = attn_total.astype(jnp.float32)
    residual = hidden_perm.astype(jnp.float32) + attn_total
    norm_mid = rms_scale(residual, ffn_gain_perm)
    gate_pre = jnp.dot(norm_mid, gate_full, preferred_element_type=jnp.float32)
    up_pre = jnp.dot(norm_mid, up_full, preferred_element_type=jnp.float32)
    hidden_ffn = (jax.nn.silu(gate_pre) * up_pre).astype(jnp.bfloat16)

    block_index = lax.broadcasted_iota(jnp.int32, (blocks, block_rows), 0)
    program_of_row = (block_index * per_block + segs).reshape(row_count)
    program_grid = lax.broadcasted_iota(jnp.int32, (programs, row_count), 0)
    selector = (program_grid == program_of_row[None, :]).astype(jnp.float32)
    hidden_sums = jnp.dot(
        selector.astype(jnp.bfloat16), hidden_ffn, preferred_element_type=jnp.float32
    )
    chunk_owner = tp_index // ratio
    owner_step = jnp.argmax(order == chunk_owner).astype(jnp.int32)
    chunk_start = owner_step * d_grp + (tp_index % ratio) * d_tp
    residual_chunk = lax.dynamic_slice_in_dim(residual, chunk_start, d_tp, 1)
    residual_sums = jnp.dot(selector, residual_chunk, precision=HIGH, preferred_element_type=jnp.float32)

    hidden_all = gather_grp(hidden_sums, chips).reshape(grp_size * programs, -1)
    down_part = lax.dot_general(
        hidden_all, down_weight.astype(jnp.float32), (((1,), (1,)), ((), ())),
        precision=HIGH, preferred_element_type=jnp.float32,
    )

    dest_all = gather_grp(dest[:, 0], chips)
    lengths_all = gather_grp(lengths.reshape(programs), chips).reshape(grp_size * programs)
    grp_ids = lax.broadcasted_iota(jnp.int32, (grp_size, programs, grp_size), 2)
    chosen = (dest_all[:, :, None] == grp_ids).astype(jnp.int32)
    earlier = jnp.cumsum(chosen, axis=1) - chosen
    slot_rank = jnp.sum(earlier * chosen, axis=2)
    slot_row = order[:, None] * capacity + slot_rank
    slots = grp_size * capacity
    target_grid = lax.broadcasted_iota(jnp.int32, (grp_size, slots, grp_size, programs), 0)
    row_grid = lax.broadcasted_iota(jnp.int32, (grp_size, slots, grp_size, programs), 1)
    placer = (
        (target_grid == dest_all[None, None]) & (row_grid == slot_row[None, None])
    ).astype(jnp.float32).reshape(grp_size, slots, grp_size * programs)
    down_slots = jnp.einsum("asq,qd->asd", placer, down_part, precision=HIGH)
    totals = jnp.zeros((slots, d_tp), jnp.float32)
    for k in range(tp_size):
        pairs = []
        for g in range(grp_size):
            for t in range(tp_size):
                u = (t - k) % tp_size
                pairs.append((g * tp_size + t, (u // ratio) * tp_size + g * ratio + u % ratio))
        u = (tp_index - k) % tp_size
        piece = lax.dynamic_index_in_dim(down_slots, u // ratio, 0, keepdims=False)
        piece = lax.dynamic_slice_in_dim(piece, (u % ratio) * d_tp, d_tp, 1)
        totals = totals + lax.ppermute(piece, ("grp", "tp"), pairs)
    local_placer = placer[:, :, :programs]
    own_rows = lax.dynamic_slice_in_dim(local_placer, grp_index * capacity, capacity, 1)
    residual_slots = jnp.einsum("asq,qd->asd", own_rows, residual_sums, precision=HIGH)
    residual_in = lax.all_to_all(residual_slots, "grp", 0, 0, tiled=True)
    totals = totals + residual_in.reshape(slots, d_tp)
    mine = lax.dynamic_index_in_dim(placer, grp_index, 0, keepdims=False)
    counts = jnp.dot(mine, lengths_all.astype(jnp.float32), precision=HIGH)
    counts = jnp.where(counts > 0, counts, 1.0)
    embedded = (totals / counts[:, None]).astype(jnp.bfloat16)
    return embedded.reshape(1, grp_size, capacity, d_tp)


def solution(mesh):
    placed = (
        P("grp", None),
        P("grp", None),
        P("grp", None),
        P(),
        P("grp", "tp"),
        P("grp", "tp"),
        P("grp", "tp"),
        P("grp", "tp"),
        P(),
        P("grp", "tp"),
        P("grp", "tp"),
        P("grp", "tp"),
    )
    return jax.shard_map(
        on_device, mesh=mesh, in_specs=placed, out_specs=P("grp", None, None, "tp"), check_vma=False
    )
```

```python
import jax
import jax.numpy as jnp
from jax import lax
from jax.sharding import PartitionSpec as P

HEAD_SIZE = 128
KVH = 4
HEADS = 16


EPSILON = 1e-06
HIGH = lax.Precision.HIGHEST


def rms_scale(rows, gain):
    rows = rows.astype(jnp.float32)
    factor = lax.rsqrt(jnp.mean(rows * rows, axis=1, keepdims=True) + EPSILON)
    return (rows * factor * gain[None, :]).astype(jnp.bfloat16)


def segment_ids(lengths, block_rows):
    bounds = jnp.cumsum(lengths, axis=1)
    position = lax.broadcasted_iota(jnp.int32, (lengths.shape[0], block_rows), 1)
    return jnp.sum((position[:, :, None] >= bounds[:, None, :]).astype(jnp.int32), axis=2)


def softmax_rows(attention_scores):
    top = jnp.max(attention_scores, axis=-1, keepdims=True)
    expo = jnp.exp(attention_scores - top)
    return (expo / jnp.sum(expo, axis=-1, keepdims=True)).astype(jnp.bfloat16)


def transposed_dot(left, right):
    return lax.dot_general(
        left, right, (((1,), (1,)), ((), ())), preferred_element_type=jnp.float32
    )


def gather_grp_halves(piece, chips):
    held = [piece]
    moving = piece
    if chips > 1:
        ring = [(2 * i + c, 2 * ((i + 1) % chips) + c) for i in range(chips) for c in range(2)]
        for _ in range(chips - 1):
            moving = lax.ppermute(moving, "grp", ring)
            held.append(moving)
    mine = jnp.stack(held)
    other = lax.ppermute(mine, "grp", [(g, g ^ 1) for g in range(2 * chips)])
    return mine.reshape(-1, piece.shape[1]), other.reshape(-1, piece.shape[1])


def halves_dot(x, halves):
    cut = halves[0].shape[0]
    first = jnp.dot(x[:, :cut], halves[0], preferred_element_type=jnp.float32)
    return first + jnp.dot(x[:, cut:], halves[1], preferred_element_type=jnp.float32)


def gather_grp(piece, chips):
    held = [piece]
    moving = piece
    if chips > 1:
        ring = [(2 * i + c, 2 * ((i + 1) % chips) + c) for i in range(chips) for c in range(2)]
        for _ in range(chips - 1):
            moving = lax.ppermute(moving, "grp", ring)
            held.append(moving)
    mine = jnp.stack(held)
    other = lax.ppermute(mine, "grp", [(g, g ^ 1) for g in range(2 * chips)])
    return jnp.concatenate([mine, other], 0)


def source_order(chips):
    g = lax.axis_index("grp")
    chip, core = g // 2, g % 2
    steps = jnp.arange(chips, dtype=jnp.int32)
    own = 2 * ((chip - steps) % chips) + core
    return jnp.concatenate([own, own - core + (1 - core)])


def take_blocks(x, order, size, axis):
    return jnp.concatenate(
        [lax.dynamic_slice_in_dim(x, order[k] * size, size, axis) for k in range(order.shape[0])],
        axis,
    )


def ring_walk(n):
    if n % 2:
        return list(range(n))
    return list(range(0, n, 2)) + list(range(n - 1, 0, -2))


def ring_psum(x, axis, n):
    walk = ring_walk(n)
    place = [0] * n
    for p, t in enumerate(walk):
        place[t] = p
    pos = jnp.asarray(place, jnp.int32)[lax.axis_index(axis)]
    rows, half = x.shape[0], x.shape[1] // 2
    size = rows // n
    parts = []
    for sign, local in ((1, x[:, :half]), (-1, x[:, half:])):
        pairs = [(walk[p], walk[(p + sign) % n]) for p in range(n)]

        def chunk(k):
            return lax.dynamic_slice_in_dim(local, ((pos - sign * k) % n) * size, size, 0)

        acc = chunk(0)
        for step in range(n - 1):
            got = lax.ppermute(acc, axis, pairs)
            acc = (got.astype(jnp.float32) + chunk(step + 1).astype(jnp.float32)).astype(x.dtype)
        out = jnp.zeros_like(local)
        moving = acc
        for step in range(n):
            if step:
                moving = lax.ppermute(moving, axis, pairs)
            where = ((pos + sign - sign * step) % n) * size
            out = lax.dynamic_update_slice_in_dim(out, moving, where, 0)
        parts.append(out)
    return jnp.concatenate(parts, 1)


def on_device(
    hidden_in,
    lengths,
    dest,
    attn_gain,
    q_weight,
    k_weight,
    v_weight,
    o_weight,
    ffn_gain,
    gate_weight,
    up_weight,
    down_weight,
):
    row_count, width = hidden_in.shape
    blocks, per_block = lengths.shape
    block_rows = row_count // blocks
    programs = blocks * per_block
    tp_size = lax.axis_size("tp")
    grp_size = lax.axis_size("grp")
    chips = grp_size // 2
    tp_index = lax.axis_index("tp")
    grp_index = lax.axis_index("grp")
    d_grp = width // grp_size
    d_tp = width // tp_size
    ratio = tp_size // grp_size
    capacity = max(2, (programs + grp_size - 1) // grp_size)
    local_heads = q_weight.shape[1] // HEAD_SIZE
    order = source_order(chips)

    q_cols, k_cols = q_weight.shape[1], k_weight.shape[1]
    qkv_full = gather_grp(jnp.concatenate([q_weight, k_weight, v_weight], 1), chips)
    qkv_full = qkv_full.reshape(width, -1)
    o_after, qkv_full = lax.optimization_barrier((o_weight, qkv_full))
    o_full = gather_grp(o_after, chips).reshape(width, -1)
    gate_after, up_after, o_full = lax.optimization_barrier((gate_weight, up_weight, o_full))
    gate_halves = gather_grp_halves(gate_after, chips)
    up_halves = gather_grp_halves(up_after, chips)

    hidden_perm = take_blocks(hidden_in, order, d_grp, 1)
    attn_gain_perm = take_blocks(attn_gain, order, d_grp, 0)
    ffn_gain_perm = take_blocks(ffn_gain, order, d_grp, 0)

    norm_in = rms_scale(hidden_perm, attn_gain_perm)
    qkv = jnp.dot(norm_in, qkv_full, preferred_element_type=jnp.float32).astype(jnp.bfloat16)
    queries = qkv[:, :q_cols]
    per_dev = k_cols // KVH
    group_heads = HEADS // KVH
    key_split = qkv[:, q_cols : q_cols + k_cols].reshape(row_count, per_dev, KVH)
    value_split = qkv[:, q_cols + k_cols :].reshape(row_count, per_dev, KVH)
    outgoing_kv = jnp.stack(
        [
            jnp.concatenate(
                [key_split[:, :, u * local_heads // group_heads], value_split[:, :, u * local_heads // group_heads]],
                1,
            )
            for u in range(tp_size)
        ]
    )
    kv_in = lax.all_to_all(outgoing_kv, "tp", 0, 0, tiled=True)
    key_head = kv_in[:, :, :per_dev].transpose(1, 0, 2).reshape(row_count, tp_size * per_dev)
    value_head = kv_in[:, :, per_dev:].transpose(1, 0, 2).reshape(row_count, tp_size * per_dev)

    segs = segment_ids(lengths, block_rows)
    same = segs[:, :, None] == segs[:, None, :]
    blocked_queries = queries.reshape(blocks, block_rows, local_heads, HEAD_SIZE)
    blocked_keys = key_head.reshape(blocks, block_rows, HEAD_SIZE)
    blocked_values = value_head.reshape(blocks, block_rows, HEAD_SIZE)
    attention_scores = jnp.einsum(
        "xwre,xpe->xrwp", blocked_queries, blocked_keys, preferred_element_type=jnp.float32
    ) * HEAD_SIZE ** (-0.5)
    attention_scores = jnp.where(same[:, None, :, :], attention_scores, -1e30)
    attention_probabilities = softmax_rows(attention_scores)
    attended_rows = jnp.einsum(
        "asfo,aon->afsn",
        attention_probabilities,
        blocked_values,
        preferred_element_type=jnp.float32,
    )
    attended_rows = attended_rows.astype(jnp.bfloat16).reshape(row_count, local_heads * HEAD_SIZE)
    attn_term = transposed_dot(attended_rows, o_full).astype(jnp.bfloat16)
    attn_total = ring_psum(attn_term, "tp", tp_size).astype(jnp.float32)
    residual = hidden_perm.astype(jnp.float32) + attn_total
    norm_mid = rms_scale(residual, ffn_gain_perm)
    gate_pre = halves_dot(norm_mid, gate_halves)
    up_pre = halves_dot(norm_mid, up_halves)
    hidden_ffn = (jax.nn.silu(gate_pre) * up_pre).astype(jnp.bfloat16)

    block_index = lax.broadcasted_iota(jnp.int32, (blocks, block_rows), 0)
    program_of_row = (block_index * per_block + segs).reshape(row_count)
    program_grid = lax.broadcasted_iota(jnp.int32, (programs, row_count), 0)
    selector = (program_grid == program_of_row[None, :]).astype(jnp.float32)
    hidden_sums = jnp.dot(
        selector.astype(jnp.bfloat16), hidden_ffn, preferred_element_type=jnp.float32
    )
    chunk_owner = tp_index // ratio
    owner_step = jnp.argmax(order == chunk_owner).astype(jnp.int32)
    chunk_start = owner_step * d_grp + (tp_index % ratio) * d_tp
    residual_chunk = lax.dynamic_slice_in_dim(residual, chunk_start, d_tp, 1)
    residual_sums = jnp.dot(selector, residual_chunk, precision=HIGH, preferred_element_type=jnp.float32)

    hidden_all = gather_grp(hidden_sums, chips).reshape(grp_size * programs, -1)
    down_part = lax.dot_general(
        hidden_all, down_weight.astype(jnp.float32), (((1,), (1,)), ((), ())),
        precision=HIGH, preferred_element_type=jnp.float32,
    )

    dest_all = gather_grp(dest[:, 0], chips)
    lengths_all = gather_grp(lengths.reshape(programs), chips).reshape(grp_size * programs)
    grp_ids = lax.broadcasted_iota(jnp.int32, (grp_size, programs, grp_size), 2)
    chosen = (dest_all[:, :, None] == grp_ids).astype(jnp.int32)
    earlier = jnp.cumsum(chosen, axis=1) - chosen
    slot_rank = jnp.sum(earlier * chosen, axis=2)
    slot_row = order[:, None] * capacity + slot_rank
    slots = grp_size * capacity
    target_grid = lax.broadcasted_iota(jnp.int32, (grp_size, slots, grp_size, programs), 0)
    row_grid = lax.broadcasted_iota(jnp.int32, (grp_size, slots, grp_size, programs), 1)
    placer = (
        (target_grid == dest_all[None, None]) & (row_grid == slot_row[None, None])
    ).astype(jnp.float32).reshape(grp_size, slots, grp_size * programs)
    down_slots = jnp.einsum("asq,qd->asd", placer, down_part, precision=HIGH)
    totals = jnp.zeros((slots, d_tp), jnp.float32)
    for k in range(tp_size):
        pairs = []
        for g in range(grp_size):
            for t in range(tp_size):
                u = (t - k) % tp_size
                pairs.append((g * tp_size + t, (u // ratio) * tp_size + g * ratio + u % ratio))
        u = (tp_index - k) % tp_size
        piece = lax.dynamic_index_in_dim(down_slots, u // ratio, 0, keepdims=False)
        piece = lax.dynamic_slice_in_dim(piece, (u % ratio) * d_tp, d_tp, 1)
        totals = totals + lax.ppermute(piece, ("grp", "tp"), pairs)
    local_placer = placer[:, :, :programs]
    own_rows = lax.dynamic_slice_in_dim(local_placer, grp_index * capacity, capacity, 1)
    residual_slots = jnp.einsum("asq,qd->asd", own_rows, residual_sums, precision=HIGH)
    residual_in = lax.all_to_all(residual_slots, "grp", 0, 0, tiled=True)
    totals = totals + residual_in.reshape(slots, d_tp)
    mine = lax.dynamic_index_in_dim(placer, grp_index, 0, keepdims=False)
    counts = jnp.dot(mine, lengths_all.astype(jnp.float32), precision=HIGH)
    counts = jnp.where(counts > 0, counts, 1.0)
    embedded = (totals / counts[:, None]).astype(jnp.bfloat16)
    return embedded.reshape(1, grp_size, capacity, d_tp)


def solution(mesh):
    placed = (
        P("grp", None),
        P("grp", None),
        P("grp", None),
        P(),
        P("grp", "tp"),
        P("grp", "tp"),
        P("grp", "tp"),
        P("grp", "tp"),
        P(),
        P("grp", "tp"),
        P("grp", "tp"),
        P("grp", "tp"),
    )
    return jax.shard_map(
        on_device, mesh=mesh, in_specs=placed, out_specs=P("grp", None, None, "tp"), check_vma=False
    )
```

```python
import jax
import jax.numpy as jnp
from jax import lax
from jax.sharding import PartitionSpec as P

HEAD_SIZE = 128
KVH = 4
HEADS = 16


EPSILON = 1e-06
HIGH = lax.Precision.HIGHEST


def rms_scale(rows, gain):
    rows = rows.astype(jnp.float32)
    factor = lax.rsqrt(jnp.mean(rows * rows, axis=1, keepdims=True) + EPSILON)
    return (rows * factor * gain[None, :]).astype(jnp.bfloat16)


def segment_ids(lengths, block_rows):
    bounds = jnp.cumsum(lengths, axis=1)
    position = lax.broadcasted_iota(jnp.int32, (lengths.shape[0], block_rows), 1)
    return jnp.sum((position[:, :, None] >= bounds[:, None, :]).astype(jnp.int32), axis=2)


def softmax_rows(attention_scores):
    top = jnp.max(attention_scores, axis=-1, keepdims=True)
    expo = jnp.exp(attention_scores - top)
    return (expo / jnp.sum(expo, axis=-1, keepdims=True)).astype(jnp.bfloat16)


def transposed_dot(left, right):
    return lax.dot_general(
        left, right, (((1,), (1,)), ((), ())), preferred_element_type=jnp.float32
    )


def gather_grp(piece, chips):
    held = [piece]
    moving = piece
    if chips > 1:
        ring = [(2 * i + c, 2 * ((i + 1) % chips) + c) for i in range(chips) for c in range(2)]
        for _ in range(chips - 1):
            moving = lax.ppermute(moving, "grp", ring)
            held.append(moving)
    mine = jnp.stack(held)
    other = lax.ppermute(mine, "grp", [(g, g ^ 1) for g in range(2 * chips)])
    return jnp.concatenate([mine, other], 0)


def source_order(chips):
    g = lax.axis_index("grp")
    chip, core = g // 2, g % 2
    steps = jnp.arange(chips, dtype=jnp.int32)
    own = 2 * ((chip - steps) % chips) + core
    return jnp.concatenate([own, own - core + (1 - core)])


def take_blocks(x, order, size, axis):
    return jnp.concatenate(
        [lax.dynamic_slice_in_dim(x, order[k] * size, size, axis) for k in range(order.shape[0])],
        axis,
    )


def ring_walk(n):
    if n % 2:
        return list(range(n))
    return list(range(0, n, 2)) + list(range(n - 1, 0, -2))


def ring_psum(x, axis, n):
    walk = ring_walk(n)
    place = [0] * n
    for p, t in enumerate(walk):
        place[t] = p
    pos = jnp.asarray(place, jnp.int32)[lax.axis_index(axis)]
    rows, half = x.shape[0], x.shape[1] // 2
    size = rows // n
    parts = []
    for sign, local in ((1, x[:, :half]), (-1, x[:, half:])):
        pairs = [(walk[p], walk[(p + sign) % n]) for p in range(n)]

        def chunk(k):
            return lax.dynamic_slice_in_dim(local, ((pos - sign * k) % n) * size, size, 0)

        acc = chunk(0)
        for step in range(n - 1):
            got = lax.ppermute(acc, axis, pairs)
            acc = (got.astype(jnp.float32) + chunk(step + 1).astype(jnp.float32)).astype(x.dtype)
        out = jnp.zeros_like(local)
        moving = acc
        for step in range(n):
            if step:
                moving = lax.ppermute(moving, axis, pairs)
            where = ((pos + sign - sign * step) % n) * size
            out = lax.dynamic_update_slice_in_dim(out, moving, where, 0)
        parts.append(out)
    return jnp.concatenate(parts, 1)


def on_device(
    hidden_in,
    lengths,
    dest,
    attn_gain,
    q_weight,
    k_weight,
    v_weight,
    o_weight,
    ffn_gain,
    gate_weight,
    up_weight,
    down_weight,
):
    row_count, width = hidden_in.shape
    blocks, per_block = lengths.shape
    block_rows = row_count // blocks
    programs = blocks * per_block
    tp_size = lax.axis_size("tp")
    grp_size = lax.axis_size("grp")
    chips = grp_size // 2
    tp_index = lax.axis_index("tp")
    grp_index = lax.axis_index("grp")
    d_grp = width // grp_size
    d_tp = width // tp_size
    ratio = tp_size // grp_size
    capacity = max(2, (programs + grp_size - 1) // grp_size)
    local_heads = q_weight.shape[1] // HEAD_SIZE
    order = source_order(chips)

    q_cols, k_cols = q_weight.shape[1], k_weight.shape[1]
    per_dev = k_cols // KVH
    group_heads = HEADS // KVH
    key_split = k_weight.reshape(d_grp, per_dev, KVH)
    value_split = v_weight.reshape(d_grp, per_dev, KVH)
    outgoing_kv = jnp.stack(
        [
            jnp.concatenate(
                [key_split[:, :, u * local_heads // group_heads], value_split[:, :, u * local_heads // group_heads]],
                1,
            )
            for u in range(tp_size)
        ]
    )
    kv_in = lax.all_to_all(outgoing_kv, "tp", 0, 0, tiled=True)
    key_cols = kv_in[:, :, :per_dev].transpose(1, 0, 2).reshape(d_grp, tp_size * per_dev)
    value_cols = kv_in[:, :, per_dev:].transpose(1, 0, 2).reshape(d_grp, tp_size * per_dev)
    q_full = gather_grp(q_weight, chips).reshape(width, -1)
    kv_full = gather_grp(jnp.concatenate([key_cols, value_cols], 1), chips).reshape(width, -1)
    o_after, q_full, kv_full = lax.optimization_barrier((o_weight, q_full, kv_full))
    o_full = gather_grp(o_after, chips).reshape(width, -1)
    gate_after, up_after, o_full = lax.optimization_barrier((gate_weight, up_weight, o_full))
    gate_full = gather_grp(gate_after, chips).reshape(width, -1)
    up_full = gather_grp(up_after, chips).reshape(width, -1)

    hidden_perm = take_blocks(hidden_in, order, d_grp, 1)
    attn_gain_perm = take_blocks(attn_gain, order, d_grp, 0)
    ffn_gain_perm = take_blocks(ffn_gain, order, d_grp, 0)

    norm_in = rms_scale(hidden_perm, attn_gain_perm)
    queries = jnp.dot(norm_in, q_full, preferred_element_type=jnp.float32).astype(jnp.bfloat16)
    kv_rows = jnp.dot(norm_in, kv_full, preferred_element_type=jnp.float32).astype(jnp.bfloat16)
    key_head = kv_rows[:, : tp_size * per_dev]
    value_head = kv_rows[:, tp_size * per_dev :]

    segs = segment_ids(lengths, block_rows)
    same = segs[:, :, None] == segs[:, None, :]
    blocked_queries = queries.reshape(blocks, block_rows, local_heads, HEAD_SIZE)
    blocked_keys = key_head.reshape(blocks, block_rows, HEAD_SIZE)
    blocked_values = value_head.reshape(blocks, block_rows, HEAD_SIZE)
    attention_scores = jnp.einsum(
        "xwre,xpe->xrwp", blocked_queries, blocked_keys, preferred_element_type=jnp.float32
    ) * HEAD_SIZE ** (-0.5)
    attention_scores = jnp.where(same[:, None, :, :], attention_scores, -1e30)
    attention_probabilities = softmax_rows(attention_scores)
    attended_rows = jnp.einsum(
        "asfo,aon->afsn",
        attention_probabilities,
        blocked_values,
        preferred_element_type=jnp.float32,
    )
    attended_rows = attended_rows.astype(jnp.bfloat16).reshape(row_count, local_heads * HEAD_SIZE)
    attn_term = transposed_dot(attended_rows, o_full).astype(jnp.bfloat16)
    attn_total = ring_psum(attn_term, "tp", tp_size).astype(jnp.float32)
    residual = hidden_perm.astype(jnp.float32) + attn_total
    norm_mid = rms_scale(residual, ffn_gain_perm)
    gate_pre = jnp.dot(norm_mid, gate_full, preferred_element_type=jnp.float32)
    up_pre = jnp.dot(norm_mid, up_full, preferred_element_type=jnp.float32)
    hidden_ffn = (jax.nn.silu(gate_pre) * up_pre).astype(jnp.bfloat16)

    block_index = lax.broadcasted_iota(jnp.int32, (blocks, block_rows), 0)
    program_of_row = (block_index * per_block + segs).reshape(row_count)
    program_grid = lax.broadcasted_iota(jnp.int32, (programs, row_count), 0)
    selector = (program_grid == program_of_row[None, :]).astype(jnp.float32)
    hidden_sums = jnp.dot(
        selector.astype(jnp.bfloat16), hidden_ffn, preferred_element_type=jnp.float32
    )
    chunk_owner = tp_index // ratio
    owner_step = jnp.argmax(order == chunk_owner).astype(jnp.int32)
    chunk_start = owner_step * d_grp + (tp_index % ratio) * d_tp
    residual_chunk = lax.dynamic_slice_in_dim(residual, chunk_start, d_tp, 1)
    residual_sums = jnp.dot(selector, residual_chunk, precision=HIGH, preferred_element_type=jnp.float32)

    hidden_all = gather_grp(hidden_sums, chips).reshape(grp_size * programs, -1)
    down_part = lax.dot_general(
        hidden_all, down_weight.astype(jnp.float32), (((1,), (1,)), ((), ())),
        precision=HIGH, preferred_element_type=jnp.float32,
    )

    dest_all = gather_grp(dest[:, 0], chips)
    lengths_all = gather_grp(lengths.reshape(programs), chips).reshape(grp_size * programs)
    grp_ids = lax.broadcasted_iota(jnp.int32, (grp_size, programs, grp_size), 2)
    chosen = (dest_all[:, :, None] == grp_ids).astype(jnp.int32)
    earlier = jnp.cumsum(chosen, axis=1) - chosen
    slot_rank = jnp.sum(earlier * chosen, axis=2)
    slot_row = order[:, None] * capacity + slot_rank
    slots = grp_size * capacity
    target_grid = lax.broadcasted_iota(jnp.int32, (grp_size, slots, grp_size, programs), 0)
    row_grid = lax.broadcasted_iota(jnp.int32, (grp_size, slots, grp_size, programs), 1)
    placer = (
        (target_grid == dest_all[None, None]) & (row_grid == slot_row[None, None])
    ).astype(jnp.float32).reshape(grp_size, slots, grp_size * programs)
    down_slots = jnp.einsum("asq,qd->asd", placer, down_part, precision=HIGH)
    totals = jnp.zeros((slots, d_tp), jnp.float32)
    for k in range(tp_size):
        pairs = []
        for g in range(grp_size):
            for t in range(tp_size):
                u = (t - k) % tp_size
                pairs.append((g * tp_size + t, (u // ratio) * tp_size + g * ratio + u % ratio))
        u = (tp_index - k) % tp_size
        piece = lax.dynamic_index_in_dim(down_slots, u // ratio, 0, keepdims=False)
        piece = lax.dynamic_slice_in_dim(piece, (u % ratio) * d_tp, d_tp, 1)
        totals = totals + lax.ppermute(piece, ("grp", "tp"), pairs)
    local_placer = placer[:, :, :programs]
    own_rows = lax.dynamic_slice_in_dim(local_placer, grp_index * capacity, capacity, 1)
    residual_slots = jnp.einsum("asq,qd->asd", own_rows, residual_sums, precision=HIGH)
    residual_in = lax.all_to_all(residual_slots, "grp", 0, 0, tiled=True)
    totals = totals + residual_in.reshape(slots, d_tp)
    mine = lax.dynamic_index_in_dim(placer, grp_index, 0, keepdims=False)
    counts = jnp.dot(mine, lengths_all.astype(jnp.float32), precision=HIGH)
    counts = jnp.where(counts > 0, counts, 1.0)
    embedded = (totals / counts[:, None]).astype(jnp.bfloat16)
    return embedded.reshape(1, grp_size, capacity, d_tp)


def solution(mesh):
    placed = (
        P("grp", None),
        P("grp", None),
        P("grp", None),
        P(),
        P("grp", "tp"),
        P("grp", "tp"),
        P("grp", "tp"),
        P("grp", "tp"),
        P(),
        P("grp", "tp"),
        P("grp", "tp"),
        P("grp", "tp"),
    )
    return jax.shard_map(
        on_device, mesh=mesh, in_specs=placed, out_specs=P("grp", None, None, "tp"), check_vma=False
    )
```

```python
import jax
import jax.numpy as jnp
from jax import lax
from jax.sharding import PartitionSpec as P

HEAD_SIZE = 128
KVH = 4
HEADS = 16


EPSILON = 1e-06
HIGH = lax.Precision.HIGHEST


def rms_scale(rows, gain):
    rows = rows.astype(jnp.float32)
    factor = lax.rsqrt(jnp.mean(rows * rows, axis=1, keepdims=True) + EPSILON)
    return (rows * factor * gain[None, :]).astype(jnp.bfloat16)


def segment_ids(lengths, block_rows):
    bounds = jnp.cumsum(lengths, axis=1)
    position = lax.broadcasted_iota(jnp.int32, (lengths.shape[0], block_rows), 1)
    return jnp.sum((position[:, :, None] >= bounds[:, None, :]).astype(jnp.int32), axis=2)


def softmax_rows(attention_scores):
    top = jnp.max(attention_scores, axis=-1, keepdims=True)
    expo = jnp.exp(attention_scores - top)
    return (expo / jnp.sum(expo, axis=-1, keepdims=True)).astype(jnp.bfloat16)


def transposed_dot(left, right):
    return lax.dot_general(
        left, right, (((1,), (1,)), ((), ())), preferred_element_type=jnp.float32
    )


def gather_grp(piece, chips):
    held = [piece]
    moving = piece
    if chips > 1:
        ring = [(2 * i + c, 2 * ((i + 1) % chips) + c) for i in range(chips) for c in range(2)]
        for _ in range(chips - 1):
            moving = lax.ppermute(moving, "grp", ring)
            held.append(moving)
    mine = jnp.stack(held)
    other = lax.ppermute(mine, "grp", [(g, g ^ 1) for g in range(2 * chips)])
    return jnp.concatenate([mine, other], 0)


def source_order(chips):
    g = lax.axis_index("grp")
    chip, core = g // 2, g % 2
    steps = jnp.arange(chips, dtype=jnp.int32)
    own = 2 * ((chip - steps) % chips) + core
    return jnp.concatenate([own, own - core + (1 - core)])


def take_blocks(x, order, size, axis):
    return jnp.concatenate(
        [lax.dynamic_slice_in_dim(x, order[k] * size, size, axis) for k in range(order.shape[0])],
        axis,
    )


def ring_walk(n):
    if n % 2:
        return list(range(n))
    return list(range(0, n, 2)) + list(range(n - 1, 0, -2))


def ring_psum(x, axis, n):
    walk = ring_walk(n)
    place = [0] * n
    for p, t in enumerate(walk):
        place[t] = p
    pos = jnp.asarray(place, jnp.int32)[lax.axis_index(axis)]
    rows, half = x.shape[0], x.shape[1] // 2
    size = rows // n
    parts = []
    for sign, local in ((1, x[:, :half]), (-1, x[:, half:])):
        pairs = [(walk[p], walk[(p + sign) % n]) for p in range(n)]

        def chunk(k):
            return lax.dynamic_slice_in_dim(local, ((pos - sign * k) % n) * size, size, 0)

        acc = chunk(0)
        for step in range(n - 1):
            got = lax.ppermute(acc, axis, pairs)
            acc = (got.astype(jnp.float32) + chunk(step + 1).astype(jnp.float32)).astype(x.dtype)
        out = jnp.zeros_like(local)
        moving = acc
        for step in range(n):
            if step:
                moving = lax.ppermute(moving, axis, pairs)
            where = ((pos + sign - sign * step) % n) * size
            out = lax.dynamic_update_slice_in_dim(out, moving, where, 0)
        parts.append(out)
    return jnp.concatenate(parts, 1)


def on_device(
    hidden_in,
    lengths,
    dest,
    attn_gain,
    q_weight,
    k_weight,
    v_weight,
    o_weight,
    ffn_gain,
    gate_weight,
    up_weight,
    down_weight,
):
    row_count, width = hidden_in.shape
    blocks, per_block = lengths.shape
    block_rows = row_count // blocks
    programs = blocks * per_block
    tp_size = lax.axis_size("tp")
    grp_size = lax.axis_size("grp")
    chips = grp_size // 2
    tp_index = lax.axis_index("tp")
    grp_index = lax.axis_index("grp")
    d_grp = width // grp_size
    d_tp = width // tp_size
    ratio = tp_size // grp_size
    capacity = max(2, (programs + grp_size - 1) // grp_size)
    local_heads = q_weight.shape[1] // HEAD_SIZE
    order = source_order(chips)

    q_cols, k_cols = q_weight.shape[1], k_weight.shape[1]
    qkv_full = gather_grp(jnp.concatenate([q_weight, k_weight, v_weight], 1), chips)
    qkv_full = qkv_full.reshape(width, -1)
    o_after, qkv_full = lax.optimization_barrier((o_weight, qkv_full))
    o_full = gather_grp(o_after, chips).reshape(width, -1)
    gate_after, up_after, o_full = lax.optimization_barrier((gate_weight, up_weight, o_full))
    gate_full = gather_grp(gate_after, chips).reshape(width, -1)
    up_full = gather_grp(up_after, chips).reshape(width, -1)

    hidden_perm = take_blocks(hidden_in, order, d_grp, 1)
    attn_gain_perm = take_blocks(attn_gain, order, d_grp, 0)
    ffn_gain_perm = take_blocks(ffn_gain, order, d_grp, 0)

    norm_in = rms_scale(hidden_perm, attn_gain_perm)
    kv = jnp.dot(norm_in, qkv_full[:, q_cols:], preferred_element_type=jnp.float32).astype(jnp.bfloat16)
    per_dev = k_cols // KVH
    group_heads = HEADS // KVH
    key_split = kv[:, :k_cols].reshape(row_count, per_dev, KVH)
    value_split = kv[:, k_cols:].reshape(row_count, per_dev, KVH)
    outgoing_kv = jnp.stack(
        [
            jnp.concatenate(
                [key_split[:, :, u * local_heads // group_heads], value_split[:, :, u * local_heads // group_heads]],
                1,
            )
            for u in range(tp_size)
        ]
    )
    kv_in = lax.all_to_all(outgoing_kv, "tp", 0, 0, tiled=True)
    queries = jnp.dot(norm_in, qkv_full[:, :q_cols], preferred_element_type=jnp.float32).astype(jnp.bfloat16)
    key_head = kv_in[:, :, :per_dev].transpose(1, 0, 2).reshape(row_count, tp_size * per_dev)
    value_head = kv_in[:, :, per_dev:].transpose(1, 0, 2).reshape(row_count, tp_size * per_dev)

    segs = segment_ids(lengths, block_rows)
    same = segs[:, :, None] == segs[:, None, :]
    blocked_queries = queries.reshape(blocks, block_rows, local_heads, HEAD_SIZE)
    blocked_keys = key_head.reshape(blocks, block_rows, HEAD_SIZE)
    blocked_values = value_head.reshape(blocks, block_rows, HEAD_SIZE)
    attention_scores = jnp.einsum(
        "xwre,xpe->xrwp", blocked_queries, blocked_keys, preferred_element_type=jnp.float32
    ) * HEAD_SIZE ** (-0.5)
    attention_scores = jnp.where(same[:, None, :, :], attention_scores, -1e30)
    attention_probabilities = softmax_rows(attention_scores)
    attended_rows = jnp.einsum(
        "asfo,aon->afsn",
        attention_probabilities,
        blocked_values,
        preferred_element_type=jnp.float32,
    )
    attended_rows = attended_rows.astype(jnp.bfloat16).reshape(row_count, local_heads * HEAD_SIZE)
    attn_term = transposed_dot(attended_rows, o_full).astype(jnp.bfloat16)
    attn_total = ring_psum(attn_term, "tp", tp_size).astype(jnp.float32)
    residual = hidden_perm.astype(jnp.float32) + attn_total
    norm_mid = rms_scale(residual, ffn_gain_perm)
    gate_pre = jnp.dot(norm_mid, gate_full, preferred_element_type=jnp.float32)
    up_pre = jnp.dot(norm_mid, up_full, preferred_element_type=jnp.float32)
    hidden_ffn = (jax.nn.silu(gate_pre) * up_pre).astype(jnp.bfloat16)

    block_index = lax.broadcasted_iota(jnp.int32, (blocks, block_rows), 0)
    program_of_row = (block_index * per_block + segs).reshape(row_count)
    program_grid = lax.broadcasted_iota(jnp.int32, (programs, row_count), 0)
    selector = (program_grid == program_of_row[None, :]).astype(jnp.float32)
    hidden_sums = jnp.dot(
        selector.astype(jnp.bfloat16), hidden_ffn, preferred_element_type=jnp.float32
    )
    chunk_owner = tp_index // ratio
    owner_step = jnp.argmax(order == chunk_owner).astype(jnp.int32)
    chunk_start = owner_step * d_grp + (tp_index % ratio) * d_tp
    residual_chunk = lax.dynamic_slice_in_dim(residual, chunk_start, d_tp, 1)
    residual_sums = jnp.dot(selector, residual_chunk, precision=HIGH, preferred_element_type=jnp.float32)

    hidden_all = gather_grp(hidden_sums, chips).reshape(grp_size * programs, -1)
    down_part = lax.dot_general(
        hidden_all, down_weight.astype(jnp.float32), (((1,), (1,)), ((), ())),
        precision=HIGH, preferred_element_type=jnp.float32,
    )

    dest_all = gather_grp(dest[:, 0], chips)
    lengths_all = gather_grp(lengths.reshape(programs), chips).reshape(grp_size * programs)
    grp_ids = lax.broadcasted_iota(jnp.int32, (grp_size, programs, grp_size), 2)
    chosen = (dest_all[:, :, None] == grp_ids).astype(jnp.int32)
    earlier = jnp.cumsum(chosen, axis=1) - chosen
    slot_rank = jnp.sum(earlier * chosen, axis=2)
    slot_row = order[:, None] * capacity + slot_rank
    slots = grp_size * capacity
    target_grid = lax.broadcasted_iota(jnp.int32, (grp_size, slots, grp_size, programs), 0)
    row_grid = lax.broadcasted_iota(jnp.int32, (grp_size, slots, grp_size, programs), 1)
    placer = (
        (target_grid == dest_all[None, None]) & (row_grid == slot_row[None, None])
    ).astype(jnp.float32).reshape(grp_size, slots, grp_size * programs)
    down_slots = jnp.einsum("asq,qd->asd", placer, down_part, precision=HIGH)
    totals = jnp.zeros((slots, d_tp), jnp.float32)
    for k in range(tp_size):
        pairs = []
        for g in range(grp_size):
            for t in range(tp_size):
                u = (t - k) % tp_size
                pairs.append((g * tp_size + t, (u // ratio) * tp_size + g * ratio + u % ratio))
        u = (tp_index - k) % tp_size
        piece = lax.dynamic_index_in_dim(down_slots, u // ratio, 0, keepdims=False)
        piece = lax.dynamic_slice_in_dim(piece, (u % ratio) * d_tp, d_tp, 1)
        totals = totals + lax.ppermute(piece, ("grp", "tp"), pairs)
    local_placer = placer[:, :, :programs]
    own_rows = lax.dynamic_slice_in_dim(local_placer, grp_index * capacity, capacity, 1)
    residual_slots = jnp.einsum("asq,qd->asd", own_rows, residual_sums, precision=HIGH)
    residual_in = lax.all_to_all(residual_slots, "grp", 0, 0, tiled=True)
    totals = totals + residual_in.reshape(slots, d_tp)
    mine = lax.dynamic_index_in_dim(placer, grp_index, 0, keepdims=False)
    counts = jnp.dot(mine, lengths_all.astype(jnp.float32), precision=HIGH)
    counts = jnp.where(counts > 0, counts, 1.0)
    embedded = (totals / counts[:, None]).astype(jnp.bfloat16)
    return embedded.reshape(1, grp_size, capacity, d_tp)


def solution(mesh):
    placed = (
        P("grp", None),
        P("grp", None),
        P("grp", None),
        P(),
        P("grp", "tp"),
        P("grp", "tp"),
        P("grp", "tp"),
        P("grp", "tp"),
        P(),
        P("grp", "tp"),
        P("grp", "tp"),
        P("grp", "tp"),
    )
    return jax.shard_map(
        on_device, mesh=mesh, in_specs=placed, out_specs=P("grp", None, None, "tp"), check_vma=False
    )
```

```python
import jax
import jax.numpy as jnp
from jax import lax
from jax.sharding import PartitionSpec as P

HEAD_SIZE = 128
KVH = 4
HEADS = 16


EPSILON = 1e-06
HIGH = lax.Precision.HIGHEST


def rms_scale(rows, gain):
    rows = rows.astype(jnp.float32)
    factor = lax.rsqrt(jnp.mean(rows * rows, axis=1, keepdims=True) + EPSILON)
    return (rows * factor * gain[None, :]).astype(jnp.bfloat16)


def segment_ids(lengths, block_rows):
    bounds = jnp.cumsum(lengths, axis=1)
    position = lax.broadcasted_iota(jnp.int32, (lengths.shape[0], block_rows), 1)
    return jnp.sum((position[:, :, None] >= bounds[:, None, :]).astype(jnp.int32), axis=2)


def softmax_rows(attention_scores):
    top = jnp.max(attention_scores, axis=-1, keepdims=True)
    expo = jnp.exp(attention_scores - top)
    return (expo / jnp.sum(expo, axis=-1, keepdims=True)).astype(jnp.bfloat16)


def transposed_dot(left, right):
    return lax.dot_general(
        left, right, (((1,), (1,)), ((), ())), preferred_element_type=jnp.float32
    )


def gather_grp(piece, chips):
    held = [piece]
    moving = piece
    if chips > 1:
        ring = [(2 * i + c, 2 * ((i + 1) % chips) + c) for i in range(chips) for c in range(2)]
        for _ in range(chips - 1):
            moving = lax.ppermute(moving, "grp", ring)
            held.append(moving)
    mine = jnp.stack(held)
    other = lax.ppermute(mine, "grp", [(g, g ^ 1) for g in range(2 * chips)])
    return jnp.concatenate([mine, other], 0)


def source_order(chips):
    g = lax.axis_index("grp")
    chip, core = g // 2, g % 2
    steps = jnp.arange(chips, dtype=jnp.int32)
    own = 2 * ((chip - steps) % chips) + core
    return jnp.concatenate([own, own - core + (1 - core)])


def take_blocks(x, order, size, axis):
    return jnp.concatenate(
        [lax.dynamic_slice_in_dim(x, order[k] * size, size, axis) for k in range(order.shape[0])],
        axis,
    )


def ring_walk(n):
    if n % 2:
        return list(range(n))
    return list(range(0, n, 2)) + list(range(n - 1, 0, -2))


def ring_psum(x, axis, n, ride):
    walk = ring_walk(n)
    place = [0] * n
    for p, t in enumerate(walk):
        place[t] = p
    pos = jnp.asarray(place, jnp.int32)[lax.axis_index(axis)]
    rows, half = x.shape[0], x.shape[1] // 2
    size = rows // n
    parts = []
    for sign, local in ((1, x[:, :half]), (-1, x[:, half:])):
        pairs = [(walk[p], walk[(p + sign) % n]) for p in range(n)]

        def chunk(k):
            return lax.dynamic_slice_in_dim(local, ((pos - sign * k) % n) * size, size, 0)

        acc = chunk(0)
        for step in range(n - 1):
            got = lax.ppermute(acc, axis, pairs)
            acc = (got.astype(jnp.float32) + chunk(step + 1).astype(jnp.float32)).astype(x.dtype)
        out = jnp.zeros_like(local)
        moving = acc
        for step in range(n):
            if step:
                moving = lax.ppermute(moving, axis, pairs)
            if step == n - 1 and sign == 1:
                moving, ride = lax.optimization_barrier((moving, ride))
            where = ((pos + sign - sign * step) % n) * size
            out = lax.dynamic_update_slice_in_dim(out, moving, where, 0)
        parts.append(out)
    return jnp.concatenate(parts, 1), ride


def on_device(
    hidden_in,
    lengths,
    dest,
    attn_gain,
    q_weight,
    k_weight,
    v_weight,
    o_weight,
    ffn_gain,
    gate_weight,
    up_weight,
    down_weight,
):
    row_count, width = hidden_in.shape
    blocks, per_block = lengths.shape
    block_rows = row_count // blocks
    programs = blocks * per_block
    tp_size = lax.axis_size("tp")
    grp_size = lax.axis_size("grp")
    chips = grp_size // 2
    tp_index = lax.axis_index("tp")
    grp_index = lax.axis_index("grp")
    d_grp = width // grp_size
    d_tp = width // tp_size
    ratio = tp_size // grp_size
    capacity = max(2, (programs + grp_size - 1) // grp_size)
    local_heads = q_weight.shape[1] // HEAD_SIZE
    order = source_order(chips)

    q_cols, k_cols = q_weight.shape[1], k_weight.shape[1]
    qkv_full = gather_grp(jnp.concatenate([q_weight, k_weight, v_weight], 1), chips)
    qkv_full = qkv_full.reshape(width, -1)
    o_after, qkv_full = lax.optimization_barrier((o_weight, qkv_full))
    o_full = gather_grp(o_after, chips).reshape(width, -1)
    gate_after, up_after, o_full = lax.optimization_barrier((gate_weight, up_weight, o_full))
    gate_full = gather_grp(gate_after, chips).reshape(width, -1)
    up_full = gather_grp(up_after, chips).reshape(width, -1)

    hidden_perm = take_blocks(hidden_in, order, d_grp, 1)
    attn_gain_perm = take_blocks(attn_gain, order, d_grp, 0)
    ffn_gain_perm = take_blocks(ffn_gain, order, d_grp, 0)

    norm_in = rms_scale(hidden_perm, attn_gain_perm)
    qkv = jnp.dot(norm_in, qkv_full, preferred_element_type=jnp.float32).astype(jnp.bfloat16)
    queries = qkv[:, :q_cols]
    per_dev = k_cols // KVH
    group_heads = HEADS // KVH
    key_split = qkv[:, q_cols : q_cols + k_cols].reshape(row_count, per_dev, KVH)
    value_split = qkv[:, q_cols + k_cols :].reshape(row_count, per_dev, KVH)
    outgoing_kv = jnp.stack(
        [
            jnp.concatenate(
                [key_split[:, :, u * local_heads // group_heads], value_split[:, :, u * local_heads // group_heads]],
                1,
            )
            for u in range(tp_size)
        ]
    )
    kv_in = lax.all_to_all(outgoing_kv, "tp", 0, 0, tiled=True)
    key_head = kv_in[:, :, :per_dev].transpose(1, 0, 2).reshape(row_count, tp_size * per_dev)
    value_head = kv_in[:, :, per_dev:].transpose(1, 0, 2).reshape(row_count, tp_size * per_dev)

    segs = segment_ids(lengths, block_rows)
    same = segs[:, :, None] == segs[:, None, :]
    blocked_queries = queries.reshape(blocks, block_rows, local_heads, HEAD_SIZE)
    blocked_keys = key_head.reshape(blocks, block_rows, HEAD_SIZE)
    blocked_values = value_head.reshape(blocks, block_rows, HEAD_SIZE)
    attention_scores = jnp.einsum(
        "xwre,xpe->xrwp", blocked_queries, blocked_keys, preferred_element_type=jnp.float32
    ) * HEAD_SIZE ** (-0.5)
    attention_scores = jnp.where(same[:, None, :, :], attention_scores, -1e30)
    attention_probabilities = softmax_rows(attention_scores)
    attended_rows = jnp.einsum(
        "asfo,aon->afsn",
        attention_probabilities,
        blocked_values,
        preferred_element_type=jnp.float32,
    )
    attended_rows = attended_rows.astype(jnp.bfloat16).reshape(row_count, local_heads * HEAD_SIZE)
    attn_term = transposed_dot(attended_rows, o_full).astype(jnp.bfloat16)
    attn_total, (gate_full, up_full) = ring_psum(attn_term, "tp", tp_size, (gate_full, up_full))
    attn_total = attn_total.astype(jnp.float32)
    residual = hidden_perm.astype(jnp.float32) + attn_total
    norm_mid = rms_scale(residual, ffn_gain_perm)
    gate_pre = jnp.dot(norm_mid, gate_full, preferred_element_type=jnp.float32)
    up_pre = jnp.dot(norm_mid, up_full, preferred_element_type=jnp.float32)
    hidden_ffn = (jax.nn.silu(gate_pre) * up_pre).astype(jnp.bfloat16)

    block_index = lax.broadcasted_iota(jnp.int32, (blocks, block_rows), 0)
    program_of_row = (block_index * per_block + segs).reshape(row_count)
    program_grid = lax.broadcasted_iota(jnp.int32, (programs, row_count), 0)
    selector = (program_grid == program_of_row[None, :]).astype(jnp.float32)
    hidden_sums = jnp.dot(
        selector.astype(jnp.bfloat16), hidden_ffn, preferred_element_type=jnp.float32
    )
    chunk_owner = tp_index // ratio
    owner_step = jnp.argmax(order == chunk_owner).astype(jnp.int32)
    chunk_start = owner_step * d_grp + (tp_index % ratio) * d_tp
    residual_chunk = lax.dynamic_slice_in_dim(residual, chunk_start, d_tp, 1)
    residual_sums = jnp.dot(selector, residual_chunk, precision=HIGH, preferred_element_type=jnp.float32)

    hidden_all = gather_grp(hidden_sums, chips).reshape(grp_size * programs, -1)
    down_part = lax.dot_general(
        hidden_all, down_weight.astype(jnp.float32), (((1,), (1,)), ((), ())),
        precision=HIGH, preferred_element_type=jnp.float32,
    )

    dest_all = gather_grp(dest[:, 0], chips)
    lengths_all = gather_grp(lengths.reshape(programs), chips).reshape(grp_size * programs)
    grp_ids = lax.broadcasted_iota(jnp.int32, (grp_size, programs, grp_size), 2)
    chosen = (dest_all[:, :, None] == grp_ids).astype(jnp.int32)
    earlier = jnp.cumsum(chosen, axis=1) - chosen
    slot_rank = jnp.sum(earlier * chosen, axis=2)
    slot_row = order[:, None] * capacity + slot_rank
    slots = grp_size * capacity
    target_grid = lax.broadcasted_iota(jnp.int32, (grp_size, slots, grp_size, programs), 0)
    row_grid = lax.broadcasted_iota(jnp.int32, (grp_size, slots, grp_size, programs), 1)
    placer = (
        (target_grid == dest_all[None, None]) & (row_grid == slot_row[None, None])
    ).astype(jnp.float32).reshape(grp_size, slots, grp_size * programs)
    down_slots = jnp.einsum("asq,qd->asd", placer, down_part, precision=HIGH)
    totals = jnp.zeros((slots, d_tp), jnp.float32)
    for k in range(tp_size):
        pairs = []
        for g in range(grp_size):
            for t in range(tp_size):
                u = (t - k) % tp_size
                pairs.append((g * tp_size + t, (u // ratio) * tp_size + g * ratio + u % ratio))
        u = (tp_index - k) % tp_size
        piece = lax.dynamic_index_in_dim(down_slots, u // ratio, 0, keepdims=False)
        piece = lax.dynamic_slice_in_dim(piece, (u % ratio) * d_tp, d_tp, 1)
        totals = totals + lax.ppermute(piece, ("grp", "tp"), pairs)
    local_placer = placer[:, :, :programs]
    own_rows = lax.dynamic_slice_in_dim(local_placer, grp_index * capacity, capacity, 1)
    residual_slots = jnp.einsum("asq,qd->asd", own_rows, residual_sums, precision=HIGH)
    residual_in = lax.all_to_all(residual_slots, "grp", 0, 0, tiled=True)
    totals = totals + residual_in.reshape(slots, d_tp)
    mine = lax.dynamic_index_in_dim(placer, grp_index, 0, keepdims=False)
    counts = jnp.dot(mine, lengths_all.astype(jnp.float32), precision=HIGH)
    counts = jnp.where(counts > 0, counts, 1.0)
    embedded = (totals / counts[:, None]).astype(jnp.bfloat16)
    return embedded.reshape(1, grp_size, capacity, d_tp)


def solution(mesh):
    placed = (
        P("grp", None),
        P("grp", None),
        P("grp", None),
        P(),
        P("grp", "tp"),
        P("grp", "tp"),
        P("grp", "tp"),
        P("grp", "tp"),
        P(),
        P("grp", "tp"),
        P("grp", "tp"),
        P("grp", "tp"),
    )
    return jax.shard_map(
        on_device, mesh=mesh, in_specs=placed, out_specs=P("grp", None, None, "tp"), check_vma=False
    )
```
